128 devices in a mesh: pairs: 8 (over x, core), win: 16 (over z, y).
Axes of the slice: x: 4, y: 4, z: 4, core: 2. Of those that a mesh axis runs over, the one named last changes fastest.
Arguments:
- records: bfloat16 [8, 96, 128, 4096], P('pairs', 'win'), may hold values from -6 to 6
- pair_list: int32 [8, 2, 2], replicated, may hold values from 0 to 7, as said below
- pair_count: int32 [8], replicated, may hold values from 1 to 2, as said below
Outputs:
- correlations: bfloat16 [8, 2, 128, 128, 128], P('pairs', None, 'win')
The draws below stay inside these ranges and needn't reach their ends.
Inputs may be any that keep to these rules, and one draw needn't show every extreme that they name: `pair_list`: the 4 block numbers in one owner's row are all distinct. `pair_count`: slots at or beyond an owner's count are unused and their correlations are zero; some owner has exactly 2 live slots and another exactly 1.
All inputs are finite; a program needn't handle non-finite values.
Results may differ from the reference program's by a relative error of at most 0.019.
Values may be sent and summed in bfloat16 or wider, within the bound.
No kernel may reach another device: no remote copies, remote signals or barrier semaphores. Data moves between devices by JAX's collectives and lax.ppermute only.
A program may use at most 128 MiB of HBM per device.

```python
import math
import jax
import jax.numpy as jnp
from jax import lax

CB = 128
NSAMP = 4096
FREQS = 32
LOW_BIN = 16
LAGS = 128
SEG_DEV = 6
SEGS = 96
BLOCKS = 8
OWNERS = 8
PAIRS_MAX = 2
N_WIN = 16


def draw_pair_list(key, part):
    owner_keys = jax.random.split(jax.random.fold_in(key, 11), OWNERS)
    lists = jax.vmap(lambda owner_key: jax.random.permutation(owner_key, BLOCKS)[:2 * PAIRS_MAX])(owner_keys)
    return lists.reshape(OWNERS, PAIRS_MAX, 2).astype(jnp.int32)


def draw_pair_count(key, part):
    count_key, busy_key, light_key = jax.random.split(jax.random.fold_in(key, 23), 3)
    lowest = PAIRS_MAX // 2
    counts = jax.random.randint(count_key, (OWNERS,), lowest, PAIRS_MAX + 1)
    busiest = jax.random.randint(busy_key, (), 0, OWNERS)
    lightest = (busiest + 1 + jax.random.randint(light_key, (), 0, OWNERS - 1)) % OWNERS
    counts = counts.at[busiest].set(PAIRS_MAX)
    counts = counts.at[lightest].set(lowest)
    return counts.astype(jnp.int32)


def block_scale(stream_key, shape, cuts, smallest, largest):
    level = 1.0
    for position, shards_of in cuts:
        heights = jax.random.uniform(jax.random.fold_in(jax.random.fold_in(stream_key, 6), position), (shards_of,), jnp.float32, smallest / len(cuts), largest / len(cuts))
        level = level * jnp.repeat(jnp.exp(heights), shape[position] // shards_of).reshape((-1,) + (1,) * (len(shape) - 1 - position))
    return level


def noise(key, dims, width, most, shards=(), kind=jnp.bfloat16):
    values = jax.random.normal(key, dims, jnp.float32) * width
    if len(shards) > 0:
        values = block_scale(key, dims, shards, -0.22, 0.18) * values
    return jnp.clip(values, min=-most, max=most).astype(kind)


def setup_inputs(seed: int = 0) -> dict:
    key_of = jax.random.split(jax.random.key(seed), 4)
    return {
        "records": noise(key_of[0], (BLOCKS, SEGS, CB, NSAMP), 1.0, 6.0, ((0, 8), (1, 16))),
        "pair_list": draw_pair_list(jax.random.fold_in(key_of[3], 71), 0),
        "pair_count": draw_pair_count(jax.random.fold_in(key_of[3], 71), 0),
    }


WATER = 0.1

def band_table():
    sample_idx = jnp.arange(NSAMP, dtype=jnp.int32)
    bin_idx = jnp.arange(FREQS, dtype=jnp.int32) + LOW_BIN
    phase = (sample_idx[:, None] * bin_idx[None, :] % NSAMP).astype(jnp.float32) * (2.0 * math.pi / NSAMP)
    scaled = jnp.concatenate([jnp.cos(phase), -jnp.sin(phase)], axis=1) * (1.0 / math.sqrt(NSAMP))
    return scaled.astype(jnp.bfloat16)

def lag_table(segments):
    bin_idx = jnp.arange(FREQS, dtype=jnp.int32) + LOW_BIN
    lag_idx = (jnp.arange(LAGS, dtype=jnp.int32) - LAGS // 2) * (NSAMP // LAGS)
    phase = (bin_idx[:, None] * lag_idx[None, :] % NSAMP).astype(jnp.float32) * (2.0 * math.pi / NSAMP)
    return jnp.concatenate([jnp.cos(phase), -jnp.sin(phase)], axis=0) * (1.0 / math.sqrt(segments * FREQS))

def whiten(spectra):
    real_part = spectra[..., :FREQS]
    imag_part = spectra[..., FREQS:]
    power_bins = real_part * real_part + imag_part * imag_part
    widths = [(0, 0)] * (power_bins.ndim - 1) + [(2, 2)]
    padded = jnp.pad(power_bins, widths)
    smooth = (padded[..., 0:FREQS] + padded[..., 1:FREQS + 1] + padded[..., 2:FREQS + 2] + padded[..., 3:FREQS + 3] + padded[..., 4:FREQS + 4]) * 0.2
    water_level = smooth + WATER * lax.optimization_barrier(jnp.mean(power_bins, axis=-1, keepdims=True)) + 1e-06
    factor = lax.rsqrt(water_level)
    return jnp.concatenate([real_part * factor, imag_part * factor], axis=-1).astype(jnp.bfloat16)

def cross_spectra(left_spec, right_spec):
    left_real = left_spec[..., :FREQS].astype(jnp.float32)
    left_imag = left_spec[..., FREQS:].astype(jnp.float32)
    right_real = right_spec[..., :FREQS].astype(jnp.float32)
    right_imag = right_spec[..., FREQS:].astype(jnp.float32)
    einsum_form = 'gsif,gsjf->gijf'
    real_sum = jnp.einsum(einsum_form, left_real, right_real) + jnp.einsum(einsum_form, left_imag, right_imag)
    imag_sum = jnp.einsum(einsum_form, left_real, right_imag) - jnp.einsum(einsum_form, left_imag, right_real)
    partial_value = jnp.concatenate([real_sum, imag_sum], axis=-1)
    rounded = lax.optimization_barrier(partial_value.astype(jnp.bfloat16))
    return lax.optimization_barrier(jnp.sum(rounded.astype(jnp.float32), axis=0))

def reference(records, pair_list, pair_count):
    table_bf = band_table()
    spectra = lax.map(lambda block_rec: whiten(jnp.dot(block_rec, table_bf, preferred_element_type=jnp.float32)), records)
    grouped = spectra.reshape(BLOCKS, N_WIN, SEG_DEV, CB, 2 * FREQS)
    lag_weights = lag_table(SEGS)

    def per_owner(owner_args):
        owner_pairs, owner_count = owner_args

        def one_pair(slot_index):
            left_spec = grouped[owner_pairs[slot_index, 0]]
            right_spec = grouped[owner_pairs[slot_index, 1]]
            stacked = cross_spectra(left_spec, right_spec)
            correlation = jnp.dot(stacked, lag_weights, precision=lax.Precision.HIGHEST, preferred_element_type=jnp.float32)
            live_slot = (slot_index < owner_count).astype(jnp.float32)
            return (correlation * live_slot).astype(jnp.bfloat16)
        return lax.map(one_pair, jnp.arange(PAIRS_MAX, dtype=jnp.int32))
    return lax.map(per_owner, (pair_list, pair_count))
```

```python
import math

import jax
import jax.numpy as jnp
import ml_dtypes
import numpy as np
from jax import lax
from jax.sharding import Mesh
from jax.sharding import PartitionSpec as P

NSAMP = 4096
FREQS = 32
LOW_BIN = 16
LAGS = 128


WATER = 0.1


def band_table():
    sample_idx = np.arange(NSAMP, dtype=np.int64)
    bin_idx = np.arange(FREQS, dtype=np.int64) + LOW_BIN
    phase = (sample_idx[:, None] * bin_idx[None, :] % NSAMP).astype(np.float64) * (
        2.0 * math.pi / NSAMP
    )
    scaled = np.concatenate([np.cos(phase), -np.sin(phase)], axis=1) * (1.0 / math.sqrt(NSAMP))
    return jnp.asarray(scaled.astype(ml_dtypes.bfloat16))


def lag_table(segments):
    bin_idx = jnp.arange(FREQS, dtype=jnp.int32) + LOW_BIN
    lag_idx = (jnp.arange(LAGS, dtype=jnp.int32) - LAGS // 2) * (NSAMP // LAGS)
    phase = (bin_idx[:, None] * lag_idx[None, :] % NSAMP).astype(jnp.float32) * (
        2.0 * math.pi / NSAMP
    )
    return jnp.concatenate([jnp.cos(phase), -jnp.sin(phase)], axis=0) * (
        1.0 / math.sqrt(segments * FREQS)
    )


def whiten(spectra):
    real_part = spectra[..., :FREQS]
    imag_part = spectra[..., FREQS:]
    power_bins = real_part * real_part + imag_part * imag_part
    widths = [(0, 0)] * (power_bins.ndim - 1) + [(2, 2)]
    padded = jnp.pad(power_bins, widths)
    smooth = (
        padded[..., 0:FREQS]
        + padded[..., 1 : FREQS + 1]
        + padded[..., 2 : FREQS + 2]
        + padded[..., 3 : FREQS + 3]
        + padded[..., 4 : FREQS + 4]
    ) * 0.2
    water_level = smooth + WATER * jnp.mean(power_bins, axis=-1, keepdims=True) + 1e-06
    factor = lax.rsqrt(water_level)
    return jnp.concatenate([real_part * factor, imag_part * factor], axis=-1).astype(jnp.bfloat16)


def shards(records, pair_list, pair_count):
    seg_dev = records.shape[1]
    block_width = records.shape[2]
    slot_count = pair_list.shape[1]
    z_count = lax.axis_size("z")
    y_count = lax.axis_size("y")
    rows = block_width // (z_count * y_count)
    spectra = whiten(jnp.dot(records[0], band_table(), preferred_element_type=jnp.float32))
    owner_index = lax.axis_index("pairs")
    y_index = lax.axis_index("y")
    every_block = lax.all_gather(spectra, "pairs", axis=0, tiled=False)
    own_pairs = lax.dynamic_index_in_dim(pair_list, owner_index, 0, keepdims=False)
    live_slots = jnp.arange(slot_count, dtype=jnp.int32) < pair_count[owner_index]
    left = jnp.take(every_block, own_pairs[:, 0], axis=0)
    right = jnp.take(every_block, own_pairs[:, 1], axis=0)
    right_all = lax.all_gather(right, "y", axis=0, tiled=False)
    left_rows = left.reshape(slot_count, seg_dev, z_count, y_count, rows, 2 * FREQS)
    left_send = jnp.transpose(left_rows, (3, 0, 1, 2, 4, 5))
    left_all = lax.all_to_all(left_send, "y", 0, 0, tiled=True)
    lr = left_all[..., :FREQS]
    li = left_all[..., FREQS:]
    rr = right_all[..., :FREQS]
    ri = right_all[..., FREQS:]
    lhs = jnp.stack([lr, li], axis=0)
    rhs_real = jnp.stack([rr, ri], axis=0)
    rhs_imag = jnp.stack([ri, -rr], axis=0)
    rhs = jnp.stack([rhs_real, rhs_imag], axis=-2)
    partial_value = jnp.einsum(
        "cyksz rf,cyksjpf->zkrjpf".replace(" ", ""),
        lhs,
        rhs,
        preferred_element_type=jnp.float32,
    )
    partial_value = partial_value.reshape(z_count, slot_count, rows, block_width, 2 * FREQS)
    stacked = lax.psum_scatter(
        partial_value.astype(jnp.bfloat16), "z", scatter_dimension=0, tiled=True
    ).astype(jnp.float32)[0]
    lag_weights = lag_table(seg_dev * z_count * y_count)
    correlation = jnp.einsum(
        "krjq,qt->krjt",
        stacked,
        lag_weights,
        precision=lax.Precision.HIGHEST,
        preferred_element_type=jnp.float32,
    )
    masked = correlation * live_slots.astype(jnp.float32)[:, None, None, None]
    return masked.astype(jnp.bfloat16)[None]


def solution(mesh):
    pairs_count, win_count = mesh.devices.shape
    y_count = 4 if win_count % 4 == 0 else 1
    grid = Mesh(
        mesh.devices.reshape(pairs_count, win_count // y_count, y_count), ("pairs", "z", "y")
    )
    in_specs = (P("pairs", ("z", "y"), None, None), P(), P())
    out_specs = P("pairs", None, ("z", "y"), None, None)
    return jax.shard_map(shards, mesh=grid, in_specs=in_specs, out_specs=out_specs, check_vma=False)
```

```python
import math

import jax
import jax.numpy as jnp
import ml_dtypes
import numpy as np
from jax import lax
from jax.sharding import Mesh
from jax.sharding import PartitionSpec as P

NSAMP = 4096
FREQS = 32
LOW_BIN = 16
LAGS = 128


WATER = 0.1


def band_table():
    sample_idx = np.arange(NSAMP, dtype=np.int64)
    bin_idx = np.arange(FREQS, dtype=np.int64) + LOW_BIN
    phase = (sample_idx[:, None] * bin_idx[None, :] % NSAMP).astype(np.float64) * (
        2.0 * math.pi / NSAMP
    )
    scaled = np.concatenate([np.cos(phase), -np.sin(phase)], axis=1) * (1.0 / math.sqrt(NSAMP))
    return jnp.asarray(scaled.astype(ml_dtypes.bfloat16))


def lag_table(segments):
    bin_idx = jnp.arange(FREQS, dtype=jnp.int32) + LOW_BIN
    lag_idx = (jnp.arange(LAGS, dtype=jnp.int32) - LAGS // 2) * (NSAMP // LAGS)
    phase = (bin_idx[:, None] * lag_idx[None, :] % NSAMP).astype(jnp.float32) * (
        2.0 * math.pi / NSAMP
    )
    return jnp.concatenate([jnp.cos(phase), -jnp.sin(phase)], axis=0) * (
        1.0 / math.sqrt(segments * FREQS)
    )


def whiten(spectra):
    real_part = spectra[..., :FREQS]
    imag_part = spectra[..., FREQS:]
    power_bins = real_part * real_part + imag_part * imag_part
    widths = [(0, 0)] * (power_bins.ndim - 1) + [(2, 2)]
    padded = jnp.pad(power_bins, widths)
    smooth = (
        padded[..., 0:FREQS]
        + padded[..., 1 : FREQS + 1]
        + padded[..., 2 : FREQS + 2]
        + padded[..., 3 : FREQS + 3]
        + padded[..., 4 : FREQS + 4]
    ) * 0.2
    water_level = smooth + WATER * jnp.mean(power_bins, axis=-1, keepdims=True) + 1e-06
    factor = lax.rsqrt(water_level)
    return jnp.concatenate([real_part * factor, imag_part * factor], axis=-1).astype(jnp.bfloat16)


def shards(records, pair_list, pair_count):
    seg_dev = records.shape[1]
    block_width = records.shape[2]
    slot_count = pair_list.shape[1]
    pairs_count = lax.axis_size("pairs")
    side = lax.axis_size("y")
    rows = block_width // (side * side)
    chips = pairs_count // 2
    half_seg = seg_dev // 2
    spectra = whiten(jnp.dot(records[0], band_table(), preferred_element_type=jnp.float32))
    own = jnp.transpose(spectra, (2, 0, 1))
    owner_index = lax.axis_index("pairs")
    core = owner_index % 2
    chip = owner_index // 2
    first_core = core == 0
    z_index = lax.axis_index("z")
    y_index = lax.axis_index("y")
    gather_pos = jnp.where(first_core, y_index, z_index)
    reduce_pos = jnp.where(first_core, z_index, y_index)

    swap = [(p, p ^ 1) for p in range(pairs_count)]
    ring = [(2 * x, 2 * ((x + 1) % chips)) for x in range(chips)] + [
        (2 * x + 1, 2 * ((x - 1) % chips) + 1) for x in range(chips)
    ]
    partner = lax.ppermute(own, "pairs", swap)
    here = jnp.where(first_core, jnp.stack([own, partner]), jnp.stack([partner, own]))
    near = lax.ppermute(here, "pairs", ring)
    relay = jnp.where(first_core, near[:, :, :half_seg], near[:, :, half_seg:])
    far_part = lax.ppermute(relay, "pairs", ring)
    other = lax.ppermute(jnp.concatenate([near, far_part], axis=2), "pairs", swap)
    other_near = other[:, :, :seg_dev]
    other_far = other[:, :, seg_dev:]
    next_chip = jnp.where(first_core, other_near, near)
    prev_chip = jnp.where(first_core, near, other_near)
    far_chip = jnp.where(
        first_core,
        jnp.concatenate([far_part, other_far], axis=2),
        jnp.concatenate([other_far, far_part], axis=2),
    )
    table = jnp.stack([here, next_chip, far_chip, prev_chip]).reshape(
        (pairs_count,) + own.shape
    )
    own_pairs = lax.dynamic_index_in_dim(pair_list, owner_index, 0, keepdims=False)
    live_slots = jnp.arange(slot_count, dtype=jnp.int32) < pair_count[owner_index]
    position = ((own_pairs // 2 - chip) % chips) * 2 + own_pairs % 2
    left = jnp.take(table, position[:, 0], axis=0)
    right = jnp.take(table, position[:, 1], axis=0)
    left6 = left.reshape(left.shape[:3] + (side, side, rows))
    left_view = jnp.where(first_core, left6, jnp.swapaxes(left6, 3, 4))

    def rows_for(pos):
        picked = lax.dynamic_index_in_dim(left_view, pos, axis=4, keepdims=False)
        return picked.reshape(picked.shape[:3] + (side * rows,))

    def gather_perm(d):
        perm = []
        for p in range(pairs_count):
            for z in range(side):
                for y in range(side):
                    src = (p * side + z) * side + y
                    if p % 2 == 0:
                        dst = (p * side + z) * side + (y + d) % side
                    else:
                        dst = (p * side + (z + d) % side) * side + y
                    perm.append((src, dst))
        return perm

    def reduce_perm(e):
        perm = []
        for p in range(pairs_count):
            for z in range(side):
                for y in range(side):
                    src = (p * side + z) * side + y
                    if p % 2 == 0:
                        dst = (p * side + (z + e) % side) * side + y
                    else:
                        dst = (p * side + z) * side + (y + e) % side
                    perm.append((src, dst))
        return perm

    axes = ("pairs", "z", "y")
    pieces = [jnp.concatenate([right, rows_for(gather_pos)], axis=-1)]
    for d in range(1, side):
        message = jnp.concatenate([right, rows_for((gather_pos + d) % side)], axis=-1)
        pieces.append(lax.ppermute(message, axes, gather_perm(d)))
    gathered = jnp.stack(pieces)
    right_all = gathered[..., :block_width]
    left_all = gathered[..., block_width:]
    lr = left_all[:, :, :FREQS]
    li = left_all[:, :, FREQS:]
    rr = right_all[:, :, :FREQS]
    ri = right_all[:, :, FREQS:]
    lhs = jnp.stack([lr, li], axis=0)
    rhs_real = jnp.stack([rr, ri], axis=0)
    rhs_imag = jnp.stack([ri, -rr], axis=0)
    rhs = jnp.stack([rhs_real, rhs_imag], axis=-2)
    partial_value = jnp.einsum(
        "cakfsm,cakfspj->kfmpj", lhs, rhs, preferred_element_type=jnp.float32
    )
    partial_value = partial_value.reshape(
        (slot_count, FREQS, side, rows, 2, block_width)
    )
    partial_value = jnp.transpose(partial_value, (2, 0, 4, 1, 3, 5)).astype(jnp.bfloat16)
    stacked = lax.dynamic_index_in_dim(partial_value, reduce_pos, 0, keepdims=False).astype(
        jnp.float32
    )
    for e in range(1, side):
        chunk = lax.dynamic_index_in_dim(partial_value, (reduce_pos + e) % side, 0, keepdims=False)
        stacked = stacked + lax.ppermute(chunk, axes, reduce_perm(e)).astype(jnp.float32)
    lag_weights = lag_table(seg_dev * side * side).reshape(2, FREQS, LAGS)
    correlation = jnp.einsum(
        "kpfrj,pft->krjt",
        stacked,
        lag_weights,
        precision=lax.Precision.HIGHEST,
        preferred_element_type=jnp.float32,
    )
    masked = correlation * live_slots.astype(jnp.float32)[:, None, None, None]
    return masked.astype(jnp.bfloat16)[None]


def solution(mesh):
    pairs_count, win_count = mesh.devices.shape
    side = math.isqrt(win_count)
    grid = Mesh(mesh.devices.reshape(pairs_count, side, side), ("pairs", "z", "y"))
    in_specs = (P("pairs", ("z", "y"), None, None), P(), P())
    out_specs = P("pairs", None, ("z", "y"), None, None)
    return jax.shard_map(shards, mesh=grid, in_specs=in_specs, out_specs=out_specs, check_vma=False)
```

```python
import math

import jax
import jax.numpy as jnp
import ml_dtypes
import numpy as np
from jax import lax
from jax.sharding import Mesh
from jax.sharding import PartitionSpec as P

NSAMP = 4096
FREQS = 32
LOW_BIN = 16
LAGS = 128


WATER = 0.1


def band_table():
    sample_idx = np.arange(NSAMP, dtype=np.int64)
    bin_idx = np.arange(FREQS, dtype=np.int64) + LOW_BIN
    phase = (sample_idx[:, None] * bin_idx[None, :] % NSAMP).astype(np.float64) * (
        2.0 * math.pi / NSAMP
    )
    scaled = np.concatenate([np.cos(phase), -np.sin(phase)], axis=1) * (1.0 / math.sqrt(NSAMP))
    return jnp.asarray(scaled.astype(ml_dtypes.bfloat16))


def lag_table(segments):
    bin_idx = jnp.arange(FREQS, dtype=jnp.int32) + LOW_BIN
    lag_idx = (jnp.arange(LAGS, dtype=jnp.int32) - LAGS // 2) * (NSAMP // LAGS)
    phase = (bin_idx[:, None] * lag_idx[None, :] % NSAMP).astype(jnp.float32) * (
        2.0 * math.pi / NSAMP
    )
    return jnp.concatenate([jnp.cos(phase), -jnp.sin(phase)], axis=0) * (
        1.0 / math.sqrt(segments * FREQS)
    )


def whiten(spectra):
    real_part = spectra[..., :FREQS]
    imag_part = spectra[..., FREQS:]
    power_bins = real_part * real_part + imag_part * imag_part
    widths = [(0, 0)] * (power_bins.ndim - 1) + [(2, 2)]
    padded = jnp.pad(power_bins, widths)
    smooth = (
        padded[..., 0:FREQS]
        + padded[..., 1 : FREQS + 1]
        + padded[..., 2 : FREQS + 2]
        + padded[..., 3 : FREQS + 3]
        + padded[..., 4 : FREQS + 4]
    ) * 0.2
    water_level = smooth + WATER * jnp.mean(power_bins, axis=-1, keepdims=True) + 1e-06
    factor = lax.rsqrt(water_level)
    return jnp.concatenate([real_part * factor, imag_part * factor], axis=-1).astype(jnp.bfloat16)


def shards(records, pair_list, pair_count):
    seg_dev = records.shape[1]
    block_width = records.shape[2]
    slot_count = pair_list.shape[1]
    pairs_count = lax.axis_size("pairs")
    side = lax.axis_size("y")
    rows = block_width // (side * side)
    chips = pairs_count // 2
    width = 2 * FREQS
    spec_rows = seg_dev * width
    half_rows = spec_rows // 2
    spectra = whiten(jnp.dot(records[0], band_table(), preferred_element_type=jnp.float32))
    own = jnp.transpose(spectra, (0, 2, 1)).reshape(spec_rows, block_width)
    owner_index = lax.axis_index("pairs")
    core = owner_index % 2
    chip = owner_index // 2
    first_core = core == 0
    z_index = lax.axis_index("z")
    y_index = lax.axis_index("y")
    gather_pos = jnp.where(first_core, y_index, z_index)
    reduce_pos = jnp.where(first_core, z_index, y_index)

    swap = [(p, p ^ 1) for p in range(pairs_count)]
    ring = [(2 * x, 2 * ((x + 1) % chips)) for x in range(chips)] + [
        (2 * x + 1, 2 * ((x - 1) % chips) + 1) for x in range(chips)
    ]
    partner = lax.ppermute(own, "pairs", swap)
    here = jnp.where(first_core, jnp.stack([own, partner]), jnp.stack([partner, own]))
    near = lax.ppermute(here, "pairs", ring)
    relay = jnp.where(first_core, near[:, :half_rows], near[:, half_rows:])
    far_part = lax.ppermute(relay, "pairs", ring)
    other = lax.ppermute(jnp.concatenate([near, far_part], axis=1), "pairs", swap)
    other_near = other[:, :spec_rows]
    other_far = other[:, spec_rows:]
    next_chip = jnp.where(first_core, other_near, near)
    prev_chip = jnp.where(first_core, near, other_near)
    far_chip = jnp.where(
        first_core,
        jnp.concatenate([far_part, other_far], axis=1),
        jnp.concatenate([other_far, far_part], axis=1),
    )
    table = jnp.stack([here, next_chip, far_chip, prev_chip]).reshape(
        (pairs_count,) + own.shape
    )
    own_pairs = lax.dynamic_index_in_dim(pair_list, owner_index, 0, keepdims=False)
    live_slots = jnp.arange(slot_count, dtype=jnp.int32) < pair_count[owner_index]
    position = ((own_pairs // 2 - chip) % chips) * 2 + own_pairs % 2
    left = jnp.take(table, position[:, 0], axis=0)
    right = jnp.take(table, position[:, 1], axis=0)
    left5 = left.reshape((slot_count, spec_rows, side, side, rows))
    left_view = jnp.where(first_core, left5, jnp.swapaxes(left5, 2, 3))
    packed_rows = spec_rows * side * rows // block_width

    def rows_for(pos):
        picked = lax.dynamic_index_in_dim(left_view, pos, axis=3, keepdims=False)
        return picked.reshape((slot_count, packed_rows, block_width))

    def gather_perm(d):
        perm = []
        for p in range(pairs_count):
            for z in range(side):
                for y in range(side):
                    src = (p * side + z) * side + y
                    if p % 2 == 0:
                        dst = (p * side + z) * side + (y + d) % side
                    else:
                        dst = (p * side + (z + d) % side) * side + y
                    perm.append((src, dst))
        return perm

    def reduce_perm(e):
        perm = []
        for p in range(pairs_count):
            for z in range(side):
                for y in range(side):
                    src = (p * side + z) * side + y
                    if p % 2 == 0:
                        dst = (p * side + (z + e) % side) * side + y
                    else:
                        dst = (p * side + z) * side + (y + e) % side
                    perm.append((src, dst))
        return perm

    axes = ("pairs", "z", "y")
    pieces = [jnp.concatenate([right, rows_for(gather_pos)], axis=1)]
    for d in range(1, side):
        message = jnp.concatenate([right, rows_for((gather_pos + d) % side)], axis=1)
        pieces.append(lax.ppermute(message, axes, gather_perm(d)))
    gathered = jnp.stack(pieces)
    right_all = gathered[:, :, :spec_rows].reshape(
        (side, slot_count, seg_dev, 2, FREQS, block_width)
    )
    left_all = gathered[:, :, spec_rows:].reshape(
        (side, slot_count, seg_dev, 2, FREQS, side * rows)
    )
    right_swapped = jnp.stack([right_all[:, :, :, 1], -right_all[:, :, :, 0]], axis=3)
    rhs = jnp.concatenate([right_all, right_swapped], axis=-1)
    partial_value = jnp.einsum(
        "akscfm,akscfn->kfmn", left_all, rhs, preferred_element_type=jnp.float32
    )
    partial_value = partial_value.reshape((slot_count, FREQS, side, rows, 2, block_width))
    partial_value = jnp.transpose(partial_value, (2, 0, 4, 1, 3, 5)).astype(jnp.bfloat16)
    chunk_rows = slot_count * 2 * FREQS * rows
    partial_value = partial_value.reshape((side, chunk_rows, block_width))
    stacked = lax.dynamic_index_in_dim(partial_value, reduce_pos, 0, keepdims=False).astype(
        jnp.float32
    )
    for e in range(1, side):
        chunk = lax.dynamic_index_in_dim(partial_value, (reduce_pos + e) % side, 0, keepdims=False)
        stacked = stacked + lax.ppermute(chunk, axes, reduce_perm(e)).astype(jnp.float32)
    stacked = stacked.reshape((slot_count, 2, FREQS, rows, block_width))
    lag_weights = lag_table(seg_dev * side * side).reshape(2, FREQS, LAGS)
    correlation = jnp.einsum(
        "kpfrj,pft->krjt",
        stacked,
        lag_weights,
        precision=lax.Precision.HIGHEST,
        preferred_element_type=jnp.float32,
    )
    masked = correlation * live_slots.astype(jnp.float32)[:, None, None, None]
    return masked.astype(jnp.bfloat16)[None]


def solution(mesh):
    pairs_count, win_count = mesh.devices.shape
    side = math.isqrt(win_count)
    grid = Mesh(mesh.devices.reshape(pairs_count, side, side), ("pairs", "z", "y"))
    in_specs = (P("pairs", ("z", "y"), None, None), P(), P())
    out_specs = P("pairs", None, ("z", "y"), None, None)
    return jax.shard_map(shards, mesh=grid, in_specs=in_specs, out_specs=out_specs, check_vma=False)
```

```python
import math

import jax
import jax.numpy as jnp
import ml_dtypes
import numpy as np
from jax import lax
from jax.sharding import Mesh
from jax.sharding import PartitionSpec as P

NSAMP = 4096
FREQS = 32
LOW_BIN = 16
LAGS = 128


WATER = 0.1


def band_table():
    sample_idx = np.arange(NSAMP, dtype=np.int64)
    bin_idx = np.arange(FREQS, dtype=np.int64) + LOW_BIN
    phase = (sample_idx[:, None] * bin_idx[None, :] % NSAMP).astype(np.float64) * (
        2.0 * math.pi / NSAMP
    )
    scaled = np.concatenate([np.cos(phase), -np.sin(phase)], axis=1) * (1.0 / math.sqrt(NSAMP))
    return jnp.asarray(scaled.astype(ml_dtypes.bfloat16))


def lag_table(segments):
    bin_idx = jnp.arange(FREQS, dtype=jnp.int32) + LOW_BIN
    lag_idx = (jnp.arange(LAGS, dtype=jnp.int32) - LAGS // 2) * (NSAMP // LAGS)
    phase = (bin_idx[:, None] * lag_idx[None, :] % NSAMP).astype(jnp.float32) * (
        2.0 * math.pi / NSAMP
    )
    return jnp.concatenate([jnp.cos(phase), -jnp.sin(phase)], axis=0) * (
        1.0 / math.sqrt(segments * FREQS)
    )


def whiten(spectra):
    real_part = spectra[..., :FREQS]
    imag_part = spectra[..., FREQS:]
    power_bins = real_part * real_part + imag_part * imag_part
    widths = [(0, 0)] * (power_bins.ndim - 1) + [(2, 2)]
    padded = jnp.pad(power_bins, widths)
    smooth = (
        padded[..., 0:FREQS]
        + padded[..., 1 : FREQS + 1]
        + padded[..., 2 : FREQS + 2]
        + padded[..., 3 : FREQS + 3]
        + padded[..., 4 : FREQS + 4]
    ) * 0.2
    water_level = smooth + WATER * jnp.mean(power_bins, axis=-1, keepdims=True) + 1e-06
    factor = lax.rsqrt(water_level)
    return jnp.concatenate([real_part * factor, imag_part * factor], axis=-1).astype(jnp.bfloat16)


def shards(records, pair_list, pair_count):
    seg_dev = records.shape[1]
    block_width = records.shape[2]
    slot_count = pair_list.shape[1]
    pairs_count = lax.axis_size("pairs")
    side = lax.axis_size("y")
    rows = block_width // (side * side)
    chips = pairs_count // 2
    width = 2 * FREQS
    spec_rows = seg_dev * width
    half_rows = spec_rows // 2
    spectra = whiten(jnp.dot(records[0], band_table(), preferred_element_type=jnp.float32))
    own = jnp.transpose(spectra, (0, 2, 1)).reshape(spec_rows, block_width)
    owner_index = lax.axis_index("pairs")
    core = owner_index % 2
    chip = owner_index // 2
    first_core = core == 0
    z_index = lax.axis_index("z")
    y_index = lax.axis_index("y")
    gather_pos = jnp.where(first_core, y_index, z_index)
    reduce_pos = jnp.where(first_core, z_index, y_index)

    swap = [(p, p ^ 1) for p in range(pairs_count)]
    chip_up = [(p, 2 * ((p // 2 + 1) % chips) + p % 2) for p in range(pairs_count)]
    chip_down = [(p, 2 * ((p // 2 - 1) % chips) + p % 2) for p in range(pairs_count)]
    partner = lax.ppermute(own, "pairs", swap)
    from_below = lax.ppermute(own, "pairs", chip_up)
    from_above = lax.ppermute(own, "pairs", chip_down)
    far_low = lax.ppermute(from_below[:half_rows], "pairs", chip_up)
    far_high = lax.ppermute(from_above[half_rows:], "pairs", chip_down)
    mine = jnp.stack([own, from_above, jnp.concatenate([far_low, far_high]), from_below])
    theirs = lax.ppermute(mine[1:], "pairs", swap)
    theirs = jnp.concatenate([partner[None], theirs])
    table = jnp.where(
        first_core, jnp.stack([mine, theirs], axis=1), jnp.stack([theirs, mine], axis=1)
    ).reshape((pairs_count,) + own.shape)
    own_pairs = lax.dynamic_index_in_dim(pair_list, owner_index, 0, keepdims=False)
    live_slots = jnp.arange(slot_count, dtype=jnp.int32) < pair_count[owner_index]
    position = ((own_pairs // 2 - chip) % chips) * 2 + own_pairs % 2
    left = jnp.take(table, position[:, 0], axis=0)
    right = jnp.take(table, position[:, 1], axis=0)
    left5 = left.reshape((slot_count, spec_rows, side, side, rows))
    left_view = jnp.where(first_core, left5, jnp.swapaxes(left5, 2, 3))
    packed_rows = spec_rows * side * rows // block_width
    packs = jnp.transpose(left_view, (3, 0, 1, 2, 4)).reshape(
        (side, slot_count, packed_rows, block_width)
    )

    def rows_for(pos):
        return lax.dynamic_index_in_dim(packs, pos % side, 0, keepdims=False)

    def axis_perm(d, gather):
        perm = []
        for p in range(pairs_count):
            along_y = (p % 2 == 0) == gather
            for z in range(side):
                for y in range(side):
                    src = (p * side + z) * side + y
                    if along_y:
                        dst = (p * side + z) * side + (y + d) % side
                    else:
                        dst = (p * side + (z + d) % side) * side + y
                    perm.append((src, dst))
        return perm

    axes = ("pairs", "z", "y")
    half_pack = packed_rows // 2
    half_spec = spec_rows // 2
    up_msg = jnp.concatenate(
        [right, rows_for(gather_pos + 1), rows_for(gather_pos + 2)[:, :half_pack]], axis=1
    )
    down_msg = jnp.concatenate(
        [right, rows_for(gather_pos - 1), rows_for(gather_pos + 2)[:, half_pack:]], axis=1
    )
    from_lower = lax.ppermute(up_msg, axes, axis_perm(1, True))
    from_upper = lax.ppermute(down_msg, axes, axis_perm(-1, True))
    relay_at = spec_rows + packed_rows
    up_msg2 = jnp.concatenate([from_lower[:, :half_spec], from_lower[:, relay_at:]], axis=1)
    down_msg2 = jnp.concatenate([from_upper[:, half_spec:spec_rows], from_upper[:, relay_at:]], axis=1)
    far_lower = lax.ppermute(up_msg2, axes, axis_perm(1, True))
    far_upper = lax.ppermute(down_msg2, axes, axis_perm(-1, True))
    far_right = jnp.concatenate([far_lower[:, :half_spec], far_upper[:, :half_spec]], axis=1)
    far_left = jnp.concatenate([far_lower[:, half_spec:], far_upper[:, half_spec:]], axis=1)
    right_all = jnp.stack(
        [right, from_lower[:, :spec_rows], from_upper[:, :spec_rows], far_right]
    )
    left_all = jnp.stack(
        [
            rows_for(gather_pos),
            from_lower[:, spec_rows:relay_at],
            from_upper[:, spec_rows:relay_at],
            far_left,
        ]
    )
    right_all = right_all.reshape((side, slot_count, seg_dev, 2, FREQS, block_width))
    left_all = left_all.reshape((side, slot_count, seg_dev, 2, FREQS, side * rows))
    right_swapped = jnp.stack([right_all[:, :, :, 1], -right_all[:, :, :, 0]], axis=3)
    rhs = jnp.concatenate([right_all, right_swapped], axis=-1)
    partial_value = jnp.einsum(
        "akscfm,akscfn->kfmn", left_all, rhs, preferred_element_type=jnp.float32
    )
    partial_value = partial_value.reshape((slot_count, FREQS, side, rows, 2, block_width))
    partial_value = jnp.transpose(partial_value, (2, 0, 4, 1, 3, 5))
    chunk_rows = slot_count * 2 * FREQS * rows
    half_chunk = chunk_rows // 2
    partial_value = partial_value.reshape((side, chunk_rows, block_width))
    partial_bf = partial_value.astype(jnp.bfloat16)

    def chunk_at(pos, values):
        return lax.dynamic_index_in_dim(values, pos % side, 0, keepdims=False)

    up_msg = jnp.concatenate(
        [chunk_at(reduce_pos + 1, partial_bf)[half_chunk:], chunk_at(reduce_pos + 2, partial_bf)[:half_chunk]]
    )
    down_msg = jnp.concatenate(
        [chunk_at(reduce_pos - 1, partial_bf)[:half_chunk], chunk_at(reduce_pos + 2, partial_bf)[half_chunk:]]
    )
    from_lower = lax.ppermute(up_msg, axes, axis_perm(1, False))
    from_upper = lax.ppermute(down_msg, axes, axis_perm(-1, False))
    up_msg2 = (
        chunk_at(reduce_pos + 1, partial_value)[:half_chunk]
        + from_lower[half_chunk:].astype(jnp.float32)
    ).astype(jnp.bfloat16)
    down_msg2 = (
        chunk_at(reduce_pos - 1, partial_value)[half_chunk:]
        + from_upper[half_chunk:].astype(jnp.float32)
    ).astype(jnp.bfloat16)
    far_lower = lax.ppermute(up_msg2, axes, axis_perm(1, False))
    far_upper = lax.ppermute(down_msg2, axes, axis_perm(-1, False))
    own_chunk = chunk_at(reduce_pos, partial_value)
    low_half = (
        own_chunk[:half_chunk]
        + from_upper[:half_chunk].astype(jnp.float32)
        + far_lower.astype(jnp.float32)
    )
    high_half = (
        own_chunk[half_chunk:]
        + from_lower[:half_chunk].astype(jnp.float32)
        + far_upper.astype(jnp.float32)
    )
    stacked = jnp.concatenate([low_half, high_half])
    stacked = stacked.reshape((slot_count, 2, FREQS, rows, block_width))
    lag_weights = lag_table(seg_dev * side * side).reshape(2, FREQS, LAGS)
    correlation = jnp.einsum(
        "kpfrj,pft->krjt",
        stacked,
        lag_weights,
        precision=lax.Precision.HIGHEST,
        preferred_element_type=jnp.float32,
    )
    masked = correlation * live_slots.astype(jnp.float32)[:, None, None, None]
    return masked.astype(jnp.bfloat16)[None]


def solution(mesh):
    pairs_count, win_count = mesh.devices.shape
    side = math.isqrt(win_count)
    grid = Mesh(mesh.devices.reshape(pairs_count, side, side), ("pairs", "z", "y"))
    in_specs = (P("pairs", ("z", "y"), None, None), P(), P())
    out_specs = P("pairs", None, ("z", "y"), None, None)
    return jax.shard_map(shards, mesh=grid, in_specs=in_specs, out_specs=out_specs, check_vma=False)
```

```python
import math

import jax
import jax.numpy as jnp
import ml_dtypes
import numpy as np
from jax import lax
from jax.sharding import Mesh
from jax.sharding import PartitionSpec as P

NSAMP = 4096
FREQS = 32
LOW_BIN = 16
LAGS = 128


WATER = 0.1


def band_table():
    sample_idx = np.arange(NSAMP, dtype=np.int64)
    bin_idx = np.arange(FREQS, dtype=np.int64) + LOW_BIN
    phase = (sample_idx[:, None] * bin_idx[None, :] % NSAMP).astype(np.float64) * (
        2.0 * math.pi / NSAMP
    )
    scaled = np.concatenate([np.cos(phase), -np.sin(phase)], axis=1) * (1.0 / math.sqrt(NSAMP))
    return jnp.asarray(scaled.astype(ml_dtypes.bfloat16))


def lag_table(segments):
    bin_idx = jnp.arange(FREQS, dtype=jnp.int32) + LOW_BIN
    lag_idx = (jnp.arange(LAGS, dtype=jnp.int32) - LAGS // 2) * (NSAMP // LAGS)
    phase = (bin_idx[:, None] * lag_idx[None, :] % NSAMP).astype(jnp.float32) * (
        2.0 * math.pi / NSAMP
    )
    return jnp.concatenate([jnp.cos(phase), -jnp.sin(phase)], axis=0) * (
        1.0 / math.sqrt(segments * FREQS)
    )


def whiten(spectra):
    real_part = spectra[..., :FREQS]
    imag_part = spectra[..., FREQS:]
    power_bins = real_part * real_part + imag_part * imag_part
    widths = [(0, 0)] * (power_bins.ndim - 1) + [(2, 2)]
    padded = jnp.pad(power_bins, widths)
    smooth = (
        padded[..., 0:FREQS]
        + padded[..., 1 : FREQS + 1]
        + padded[..., 2 : FREQS + 2]
        + padded[..., 3 : FREQS + 3]
        + padded[..., 4 : FREQS + 4]
    ) * 0.2
    water_level = smooth + WATER * jnp.mean(power_bins, axis=-1, keepdims=True) + 1e-06
    factor = lax.rsqrt(water_level)
    return jnp.concatenate([real_part * factor, imag_part * factor], axis=-1).astype(jnp.bfloat16)


def shards(records, pair_list, pair_count):
    seg_dev = records.shape[1]
    block_width = records.shape[2]
    slot_count = pair_list.shape[1]
    pairs_count = lax.axis_size("pairs")
    side = lax.axis_size("y")
    rows = block_width // (side * side)
    chips = pairs_count // 2
    width = 2 * FREQS
    spec_rows = seg_dev * width
    half_rows = spec_rows // 2
    spectra = whiten(jnp.dot(records[0], band_table(), preferred_element_type=jnp.float32))
    own = jnp.transpose(spectra, (0, 2, 1)).reshape(spec_rows, block_width)
    owner_index = lax.axis_index("pairs")
    core = owner_index % 2
    chip = owner_index // 2
    first_core = core == 0
    z_index = lax.axis_index("z")
    y_index = lax.axis_index("y")
    gather_pos = jnp.where(first_core, y_index, z_index)
    reduce_pos = jnp.where(first_core, z_index, y_index)

    swap = [(p, p ^ 1) for p in range(pairs_count)]

    def chip_shift(d):
        return [(p, 2 * ((p // 2 + d) % chips) + p % 2) for p in range(pairs_count)]

    partner = lax.ppermute(own, "pairs", swap)
    from_below = lax.ppermute(own, "pairs", chip_shift(1))
    from_above = lax.ppermute(own, "pairs", chip_shift(-1))
    from_far = lax.ppermute(own, "pairs", chip_shift(2))
    mine = jnp.stack([own, from_above, from_far, from_below])
    theirs = lax.ppermute(mine[1:], "pairs", swap)
    theirs = jnp.concatenate([partner[None], theirs])
    table = jnp.where(
        first_core, jnp.stack([mine, theirs], axis=1), jnp.stack([theirs, mine], axis=1)
    ).reshape((pairs_count,) + own.shape)
    own_pairs = lax.dynamic_index_in_dim(pair_list, owner_index, 0, keepdims=False)
    live_slots = jnp.arange(slot_count, dtype=jnp.int32) < pair_count[owner_index]
    position = ((own_pairs // 2 - chip) % chips) * 2 + own_pairs % 2
    left = jnp.take(table, position[:, 0], axis=0)
    right = jnp.take(table, position[:, 1], axis=0)
    left_t = jnp.transpose(left, (0, 2, 1)).reshape((slot_count, side, side, rows, spec_rows))
    left_t = jnp.where(first_core, jnp.swapaxes(left_t, 1, 2), left_t)
    packed_rows = spec_rows * side * rows // block_width
    packs = jnp.transpose(left_t, (1, 0, 2, 3, 4)).reshape(
        (side, slot_count, packed_rows, block_width)
    )

    def rows_for(pos):
        return lax.dynamic_index_in_dim(packs, pos, 0, keepdims=False)

    def gather_perm(d):
        perm = []
        for p in range(pairs_count):
            for z in range(side):
                for y in range(side):
                    src = (p * side + z) * side + y
                    if p % 2 == 0:
                        dst = (p * side + z) * side + (y + d) % side
                    else:
                        dst = (p * side + (z + d) % side) * side + y
                    perm.append((src, dst))
        return perm

    def reduce_perm(e):
        perm = []
        for p in range(pairs_count):
            for z in range(side):
                for y in range(side):
                    src = (p * side + z) * side + y
                    if p % 2 == 0:
                        dst = (p * side + (z + e) % side) * side + y
                    else:
                        dst = (p * side + z) * side + (y + e) % side
                    perm.append((src, dst))
        return perm

    axes = ("pairs", "z", "y")
    pieces = [jnp.concatenate([right, rows_for(gather_pos)], axis=1)]
    for d in range(1, side):
        message = jnp.concatenate([right, rows_for((gather_pos + d) % side)], axis=1)
        pieces.append(lax.ppermute(message, axes, gather_perm(d)))
    gathered = jnp.stack(pieces)
    right_all = gathered[:, :, :spec_rows].reshape(
        (side, slot_count, seg_dev, 2, FREQS, block_width)
    )
    left_all = gathered[:, :, spec_rows:].reshape((side, slot_count, side * rows, seg_dev, 2, FREQS))
    left_all = jnp.transpose(left_all, (0, 1, 3, 4, 5, 2))
    right_swapped = jnp.stack([right_all[:, :, :, 1], -right_all[:, :, :, 0]], axis=3)
    rhs = jnp.concatenate([right_all, right_swapped], axis=-1)
    partial_value = jnp.einsum(
        "akscfm,akscfn->kfmn", left_all, rhs, preferred_element_type=jnp.float32
    )
    partial_value = partial_value.reshape((slot_count, FREQS, side, rows, 2, block_width))
    partial_value = jnp.transpose(partial_value, (2, 0, 4, 1, 3, 5)).astype(jnp.bfloat16)
    chunk_rows = slot_count * 2 * FREQS * rows
    partial_value = partial_value.reshape((side, chunk_rows, block_width))
    stacked = lax.dynamic_index_in_dim(partial_value, reduce_pos, 0, keepdims=False).astype(
        jnp.float32
    )
    for e in range(1, side):
        chunk = lax.dynamic_index_in_dim(partial_value, (reduce_pos + e) % side, 0, keepdims=False)
        stacked = stacked + lax.ppermute(chunk, axes, reduce_perm(e)).astype(jnp.float32)
    stacked = stacked.reshape((slot_count, 2, FREQS, rows, block_width))
    lag_weights = lag_table(seg_dev * side * side).reshape(2, FREQS, LAGS)
    correlation = jnp.einsum(
        "kpfrj,pft->krjt",
        stacked,
        lag_weights,
        precision=lax.Precision.HIGHEST,
        preferred_element_type=jnp.float32,
    )
    masked = correlation * live_slots.astype(jnp.float32)[:, None, None, None]
    return masked.astype(jnp.bfloat16)[None]


def solution(mesh):
    pairs_count, win_count = mesh.devices.shape
    side = math.isqrt(win_count)
    grid = Mesh(mesh.devices.reshape(pairs_count, side, side), ("pairs", "z", "y"))
    in_specs = (P("pairs", ("z", "y"), None, None), P(), P())
    out_specs = P("pairs", None, ("z", "y"), None, None)
    return jax.shard_map(shards, mesh=grid, in_specs=in_specs, out_specs=out_specs, check_vma=False)
```

```python
import math

import jax
import jax.numpy as jnp
import ml_dtypes
import numpy as np
from jax import lax
from jax.experimental import pallas as pl
from jax.sharding import Mesh
from jax.sharding import PartitionSpec as P

NSAMP = 4096
FREQS = 32
LOW_BIN = 16
LAGS = 128


WATER = 0.1


def band_table():
    sample_idx = np.arange(NSAMP, dtype=np.int64)
    bin_idx = np.arange(FREQS, dtype=np.int64) + LOW_BIN
    phase = (sample_idx[:, None] * bin_idx[None, :] % NSAMP).astype(np.float64) * (
        2.0 * math.pi / NSAMP
    )
    scaled = np.concatenate([np.cos(phase), -np.sin(phase)], axis=1) * (1.0 / math.sqrt(NSAMP))
    return jnp.asarray(scaled.astype(ml_dtypes.bfloat16))


def lag_table(segments):
    bin_idx = jnp.arange(FREQS, dtype=jnp.int32) + LOW_BIN
    lag_idx = (jnp.arange(LAGS, dtype=jnp.int32) - LAGS // 2) * (NSAMP // LAGS)
    phase = (bin_idx[:, None] * lag_idx[None, :] % NSAMP).astype(jnp.float32) * (
        2.0 * math.pi / NSAMP
    )
    return jnp.concatenate([jnp.cos(phase), -jnp.sin(phase)], axis=0) * (
        1.0 / math.sqrt(segments * FREQS)
    )


def project_kernel(x_ref, table_ref, out_ref):
    out_ref[...] = jnp.dot(x_ref[...], table_ref[...], preferred_element_type=jnp.float32)


def band_project(samples):
    count = samples.shape[0]
    tile = 128
    width = 2 * FREQS
    return pl.pallas_call(
        project_kernel,
        out_shape=jax.ShapeDtypeStruct((count, width), jnp.float32),
        grid=(count // tile,),
        in_specs=[
            pl.BlockSpec((tile, NSAMP), lambda i: (i, 0)),
            pl.BlockSpec((NSAMP, width), lambda i: (0, 0)),
        ],
        out_specs=pl.BlockSpec((tile, width), lambda i: (i, 0)),
        cost_estimate=pl.CostEstimate(
            flops=2 * count * NSAMP * width,
            transcendentals=0,
            bytes_accessed=count * NSAMP * 2 + NSAMP * width * 2 + count * width * 4,
        ),
    )(samples, band_table())


def whiten(spectra):
    real_part = spectra[..., :FREQS]
    imag_part = spectra[..., FREQS:]
    power_bins = real_part * real_part + imag_part * imag_part
    widths = [(0, 0)] * (power_bins.ndim - 1) + [(2, 2)]
    padded = jnp.pad(power_bins, widths)
    smooth = (
        padded[..., 0:FREQS]
        + padded[..., 1 : FREQS + 1]
        + padded[..., 2 : FREQS + 2]
        + padded[..., 3 : FREQS + 3]
        + padded[..., 4 : FREQS + 4]
    ) * 0.2
    water_level = smooth + WATER * jnp.mean(power_bins, axis=-1, keepdims=True) + 1e-06
    factor = lax.rsqrt(water_level)
    return jnp.concatenate([real_part * factor, imag_part * factor], axis=-1).astype(jnp.bfloat16)


def shards(records, pair_list, pair_count):
    seg_dev = records.shape[1]
    block_width = records.shape[2]
    slot_count = pair_list.shape[1]
    pairs_count = lax.axis_size("pairs")
    side = lax.axis_size("y")
    rows = block_width // (side * side)
    chips = pairs_count // 2
    width = 2 * FREQS
    spec_rows = seg_dev * width
    half_rows = spec_rows // 2
    samples = records[0].reshape(seg_dev * block_width, NSAMP)
    spectra = whiten(band_project(samples)).reshape(seg_dev, block_width, 2 * FREQS)
    own = jnp.transpose(spectra, (0, 2, 1)).reshape(spec_rows, block_width)
    owner_index = lax.axis_index("pairs")
    core = owner_index % 2
    chip = owner_index // 2
    first_core = core == 0
    z_index = lax.axis_index("z")
    y_index = lax.axis_index("y")
    gather_pos = jnp.where(first_core, y_index, z_index)
    reduce_pos = jnp.where(first_core, z_index, y_index)

    swap = [(p, p ^ 1) for p in range(pairs_count)]

    def chip_shift(d):
        return [(p, 2 * ((p // 2 + d) % chips) + p % 2) for p in range(pairs_count)]

    partner = lax.ppermute(own, "pairs", swap)
    from_below = lax.ppermute(own, "pairs", chip_shift(1))
    from_above = lax.ppermute(own, "pairs", chip_shift(-1))
    from_far = lax.ppermute(own, "pairs", chip_shift(2))
    mine = jnp.stack([own, from_above, from_far, from_below])
    theirs = lax.ppermute(mine[1:], "pairs", swap)
    theirs = jnp.concatenate([partner[None], theirs])
    table = jnp.where(
        first_core, jnp.stack([mine, theirs], axis=1), jnp.stack([theirs, mine], axis=1)
    ).reshape((pairs_count,) + own.shape)
    own_pairs = lax.dynamic_index_in_dim(pair_list, owner_index, 0, keepdims=False)
    live_slots = jnp.arange(slot_count, dtype=jnp.int32) < pair_count[owner_index]
    position = ((own_pairs // 2 - chip) % chips) * 2 + own_pairs % 2
    left = jnp.take(table, position[:, 0], axis=0)
    right = jnp.take(table, position[:, 1], axis=0)
    left_t = jnp.transpose(left, (0, 2, 1)).reshape((slot_count, side, side, rows, spec_rows))
    left_t = jnp.where(first_core, jnp.swapaxes(left_t, 1, 2), left_t)
    packed_rows = spec_rows * side * rows // block_width
    packs = jnp.transpose(left_t, (1, 0, 2, 3, 4)).reshape(
        (side, slot_count, packed_rows, block_width)
    )

    def rows_for(pos):
        return lax.dynamic_index_in_dim(packs, pos, 0, keepdims=False)

    def gather_perm(d):
        perm = []
        for p in range(pairs_count):
            for z in range(side):
                for y in range(side):
                    src = (p * side + z) * side + y
                    if p % 2 == 0:
                        dst = (p * side + z) * side + (y + d) % side
                    else:
                        dst = (p * side + (z + d) % side) * side + y
                    perm.append((src, dst))
        return perm

    def reduce_perm(e):
        perm = []
        for p in range(pairs_count):
            for z in range(side):
                for y in range(side):
                    src = (p * side + z) * side + y
                    if p % 2 == 0:
                        dst = (p * side + (z + e) % side) * side + y
                    else:
                        dst = (p * side + z) * side + (y + e) % side
                    perm.append((src, dst))
        return perm

    axes = ("pairs", "z", "y")
    pieces = [jnp.concatenate([right, rows_for(gather_pos)], axis=1)]
    for d in range(1, side):
        message = jnp.concatenate([right, rows_for((gather_pos + d) % side)], axis=1)
        pieces.append(lax.ppermute(message, axes, gather_perm(d)))
    gathered = jnp.stack(pieces)
    right_all = gathered[:, :, :spec_rows].reshape(
        (side, slot_count, seg_dev, 2, FREQS, block_width)
    )
    left_all = gathered[:, :, spec_rows:].reshape((side, slot_count, side * rows, seg_dev, 2, FREQS))
    left_all = jnp.transpose(left_all, (0, 1, 3, 4, 5, 2))
    right_swapped = jnp.stack([right_all[:, :, :, 1], -right_all[:, :, :, 0]], axis=3)
    rhs = jnp.concatenate([right_all, right_swapped], axis=-1)
    partial_value = jnp.einsum(
        "akscfm,akscfn->kfmn", left_all, rhs, preferred_element_type=jnp.float32
    )
    partial_value = partial_value.reshape((slot_count, FREQS, side, rows, 2, block_width))
    partial_value = jnp.transpose(partial_value, (2, 0, 4, 1, 3, 5)).astype(jnp.bfloat16)
    chunk_rows = slot_count * 2 * FREQS * rows
    partial_value = partial_value.reshape((side, chunk_rows, block_width))
    stacked = lax.dynamic_index_in_dim(partial_value, reduce_pos, 0, keepdims=False).astype(
        jnp.float32
    )
    for e in range(1, side):
        chunk = lax.dynamic_index_in_dim(partial_value, (reduce_pos + e) % side, 0, keepdims=False)
        stacked = stacked + lax.ppermute(chunk, axes, reduce_perm(e)).astype(jnp.float32)
    stacked = stacked.reshape((slot_count, 2, FREQS, rows, block_width))
    lag_weights = lag_table(seg_dev * side * side).reshape(2, FREQS, LAGS)
    correlation = jnp.einsum(
        "kpfrj,pft->krjt",
        stacked,
        lag_weights,
        precision=lax.Precision.HIGH,
        preferred_element_type=jnp.float32,
    )
    masked = correlation * live_slots.astype(jnp.float32)[:, None, None, None]
    return masked.astype(jnp.bfloat16)[None]


def solution(mesh):
    pairs_count, win_count = mesh.devices.shape
    side = math.isqrt(win_count)
    grid = Mesh(mesh.devices.reshape(pairs_count, side, side), ("pairs", "z", "y"))
    in_specs = (P("pairs", ("z", "y"), None, None), P(), P())
    out_specs = P("pairs", None, ("z", "y"), None, None)
    return jax.shard_map(shards, mesh=grid, in_specs=in_specs, out_specs=out_specs, check_vma=False)
```

```python
import math

import jax
import jax.numpy as jnp
import ml_dtypes
import numpy as np
from jax import lax
from jax.experimental.layout import Layout, with_layout_constraint
from jax.sharding import Mesh
from jax.sharding import PartitionSpec as P

NSAMP = 4096
FREQS = 32
LOW_BIN = 16
LAGS = 128


WATER = 0.1


def band_table():
    sample_idx = np.arange(NSAMP, dtype=np.int64)
    bin_idx = np.arange(FREQS, dtype=np.int64) + LOW_BIN
    phase = (sample_idx[:, None] * bin_idx[None, :] % NSAMP).astype(np.float64) * (
        2.0 * math.pi / NSAMP
    )
    scaled = np.concatenate([np.cos(phase), -np.sin(phase)], axis=1) * (1.0 / math.sqrt(NSAMP))
    return jnp.asarray(scaled.astype(ml_dtypes.bfloat16))


def lag_table(segments):
    bin_idx = jnp.arange(FREQS, dtype=jnp.int32) + LOW_BIN
    lag_idx = (jnp.arange(LAGS, dtype=jnp.int32) - LAGS // 2) * (NSAMP // LAGS)
    phase = (bin_idx[:, None] * lag_idx[None, :] % NSAMP).astype(jnp.float32) * (
        2.0 * math.pi / NSAMP
    )
    return jnp.concatenate([jnp.cos(phase), -jnp.sin(phase)], axis=0) * (
        1.0 / math.sqrt(segments * FREQS)
    )


def whiten(spectra):
    real_part = spectra[..., :FREQS]
    imag_part = spectra[..., FREQS:]
    power_bins = real_part * real_part + imag_part * imag_part
    widths = [(0, 0)] * (power_bins.ndim - 1) + [(2, 2)]
    padded = jnp.pad(power_bins, widths)
    smooth = (
        padded[..., 0:FREQS]
        + padded[..., 1 : FREQS + 1]
        + padded[..., 2 : FREQS + 2]
        + padded[..., 3 : FREQS + 3]
        + padded[..., 4 : FREQS + 4]
    ) * 0.2
    water_level = smooth + WATER * jnp.mean(power_bins, axis=-1, keepdims=True) + 1e-06
    factor = lax.rsqrt(water_level)
    return jnp.concatenate([real_part * factor, imag_part * factor], axis=-1).astype(jnp.bfloat16)


def shards(records, pair_list, pair_count):
    seg_dev = records.shape[1]
    block_width = records.shape[2]
    slot_count = pair_list.shape[1]
    pairs_count = lax.axis_size("pairs")
    side = lax.axis_size("y")
    rows = block_width // (side * side)
    chips = pairs_count // 2
    width = 2 * FREQS
    spec_rows = seg_dev * width
    half_rows = spec_rows // 2
    samples = records[0].reshape(seg_dev * block_width, NSAMP)
    projected = with_layout_constraint(
        jnp.dot(samples, band_table(), preferred_element_type=jnp.float32), Layout((0, 1))
    )
    spectra = whiten(projected).reshape(seg_dev, block_width, 2 * FREQS)
    own = jnp.transpose(spectra, (0, 2, 1)).reshape(spec_rows, block_width)
    owner_index = lax.axis_index("pairs")
    core = owner_index % 2
    chip = owner_index // 2
    first_core = core == 0
    z_index = lax.axis_index("z")
    y_index = lax.axis_index("y")
    gather_pos = jnp.where(first_core, y_index, z_index)
    reduce_pos = jnp.where(first_core, z_index, y_index)

    swap = [(p, p ^ 1) for p in range(pairs_count)]

    def chip_shift(d):
        return [(p, 2 * ((p // 2 + d) % chips) + p % 2) for p in range(pairs_count)]

    partner = lax.ppermute(own, "pairs", swap)
    from_below = lax.ppermute(own, "pairs", chip_shift(1))
    from_above = lax.ppermute(own, "pairs", chip_shift(-1))
    from_far = lax.ppermute(own, "pairs", chip_shift(2))
    mine = jnp.stack([own, from_above, from_far, from_below])
    theirs = lax.ppermute(mine[1:], "pairs", swap)
    theirs = jnp.concatenate([partner[None], theirs])
    table = jnp.where(
        first_core, jnp.stack([mine, theirs], axis=1), jnp.stack([theirs, mine], axis=1)
    ).reshape((pairs_count,) + own.shape)
    own_pairs = lax.dynamic_index_in_dim(pair_list, owner_index, 0, keepdims=False)
    live_slots = jnp.arange(slot_count, dtype=jnp.int32) < pair_count[owner_index]
    position = ((own_pairs // 2 - chip) % chips) * 2 + own_pairs % 2
    left = jnp.take(table, position[:, 0], axis=0)
    right = jnp.take(table, position[:, 1], axis=0)
    left_t = jnp.transpose(left, (0, 2, 1)).reshape((slot_count, side, side, rows, spec_rows))
    left_t = jnp.where(first_core, jnp.swapaxes(left_t, 1, 2), left_t)
    packed_rows = spec_rows * side * rows // block_width
    packs = jnp.transpose(left_t, (1, 0, 2, 3, 4)).reshape(
        (side, slot_count, packed_rows, block_width)
    )

    def rows_for(pos):
        return lax.dynamic_index_in_dim(packs, pos, 0, keepdims=False)

    def gather_perm(d):
        perm = []
        for p in range(pairs_count):
            for z in range(side):
                for y in range(side):
                    src = (p * side + z) * side + y
                    if p % 2 == 0:
                        dst = (p * side + z) * side + (y + d) % side
                    else:
                        dst = (p * side + (z + d) % side) * side + y
                    perm.append((src, dst))
        return perm

    def reduce_perm(e):
        perm = []
        for p in range(pairs_count):
            for z in range(side):
                for y in range(side):
                    src = (p * side + z) * side + y
                    if p % 2 == 0:
                        dst = (p * side + (z + e) % side) * side + y
                    else:
                        dst = (p * side + z) * side + (y + e) % side
                    perm.append((src, dst))
        return perm

    axes = ("pairs", "z", "y")
    pieces = [jnp.concatenate([right, rows_for(gather_pos)], axis=1)]
    for d in range(1, side):
        message = jnp.concatenate([right, rows_for((gather_pos + d) % side)], axis=1)
        pieces.append(lax.ppermute(message, axes, gather_perm(d)))
    gathered = jnp.stack(pieces)
    right_all = gathered[:, :, :spec_rows].reshape(
        (side, slot_count, seg_dev, 2, FREQS, block_width)
    )
    left_all = gathered[:, :, spec_rows:].reshape((side, slot_count, side * rows, seg_dev, 2, FREQS))
    left_all = jnp.transpose(left_all, (0, 1, 3, 4, 5, 2))
    right_swapped = jnp.stack([right_all[:, :, :, 1], -right_all[:, :, :, 0]], axis=3)
    rhs = jnp.concatenate([right_all, right_swapped], axis=-1)
    partial_value = jnp.einsum(
        "akscfm,akscfn->kfmn", left_all, rhs, preferred_element_type=jnp.float32
    )
    partial_value = partial_value.reshape((slot_count, FREQS, side, rows, 2, block_width))
    partial_value = jnp.transpose(partial_value, (2, 0, 4, 1, 3, 5)).astype(jnp.bfloat16)
    chunk_rows = slot_count * 2 * FREQS * rows
    partial_value = partial_value.reshape((side, chunk_rows, block_width))
    stacked = lax.dynamic_index_in_dim(partial_value, reduce_pos, 0, keepdims=False).astype(
        jnp.float32
    )
    for e in range(1, side):
        chunk = lax.dynamic_index_in_dim(partial_value, (reduce_pos + e) % side, 0, keepdims=False)
        stacked = stacked + lax.ppermute(chunk, axes, reduce_perm(e)).astype(jnp.float32)
    stacked = stacked.reshape((slot_count, 2, FREQS, rows, block_width))
    lag_weights = lag_table(seg_dev * side * side).reshape(2, FREQS, LAGS)
    correlation = jnp.einsum(
        "kpfrj,pft->krjt",
        stacked,
        lag_weights,
        precision=lax.Precision.HIGH,
        preferred_element_type=jnp.float32,
    )
    masked = correlation * live_slots.astype(jnp.float32)[:, None, None, None]
    return masked.astype(jnp.bfloat16)[None]


def solution(mesh):
    pairs_count, win_count = mesh.devices.shape
    side = math.isqrt(win_count)
    grid = Mesh(mesh.devices.reshape(pairs_count, side, side), ("pairs", "z", "y"))
    in_specs = (P("pairs", ("z", "y"), None, None), P(), P())
    out_specs = P("pairs", None, ("z", "y"), None, None)
    return jax.shard_map(shards, mesh=grid, in_specs=in_specs, out_specs=out_specs, check_vma=False)
```

```python
import math

import jax
import jax.numpy as jnp
import ml_dtypes
import numpy as np
from jax import lax
from jax.experimental.layout import Layout, with_layout_constraint
from jax.sharding import Mesh
from jax.sharding import PartitionSpec as P

NSAMP = 4096
FREQS = 32
LOW_BIN = 16
LAGS = 128


WATER = 0.1


def band_table():
    sample_idx = np.arange(NSAMP, dtype=np.int64)
    bin_idx = np.arange(FREQS, dtype=np.int64) + LOW_BIN
    phase = (sample_idx[:, None] * bin_idx[None, :] % NSAMP).astype(np.float64) * (
        2.0 * math.pi / NSAMP
    )
    scaled = np.concatenate([np.cos(phase), -np.sin(phase)], axis=1) * (1.0 / math.sqrt(NSAMP))
    return jnp.asarray(scaled.astype(ml_dtypes.bfloat16))


def lag_table(segments):
    bin_idx = jnp.arange(FREQS, dtype=jnp.int32) + LOW_BIN
    lag_idx = (jnp.arange(LAGS, dtype=jnp.int32) - LAGS // 2) * (NSAMP // LAGS)
    phase = (bin_idx[:, None] * lag_idx[None, :] % NSAMP).astype(jnp.float32) * (
        2.0 * math.pi / NSAMP
    )
    return jnp.concatenate([jnp.cos(phase), -jnp.sin(phase)], axis=0) * (
        1.0 / math.sqrt(segments * FREQS)
    )


def whiten(spectra):
    real_part = spectra[..., :FREQS]
    imag_part = spectra[..., FREQS:]
    power_bins = real_part * real_part + imag_part * imag_part
    widths = [(0, 0)] * (power_bins.ndim - 1) + [(2, 2)]
    padded = jnp.pad(power_bins, widths)
    smooth = (
        padded[..., 0:FREQS]
        + padded[..., 1 : FREQS + 1]
        + padded[..., 2 : FREQS + 2]
        + padded[..., 3 : FREQS + 3]
        + padded[..., 4 : FREQS + 4]
    ) * 0.2
    water_level = smooth + WATER * jnp.mean(power_bins, axis=-1, keepdims=True) + 1e-06
    factor = lax.rsqrt(water_level)
    return jnp.concatenate([real_part * factor, imag_part * factor], axis=-1).astype(jnp.bfloat16)


def shards(records, pair_list, pair_count):
    seg_dev = records.shape[1]
    block_width = records.shape[2]
    slot_count = pair_list.shape[1]
    pairs_count = lax.axis_size("pairs")
    side = lax.axis_size("y")
    rows = block_width // (side * side)
    chips = pairs_count // 2
    width = 2 * FREQS
    spec_rows = seg_dev * width
    half_rows = spec_rows // 2
    samples = records[0].reshape(seg_dev * block_width, NSAMP)
    projected = with_layout_constraint(
        jnp.dot(samples, band_table(), preferred_element_type=jnp.float32), Layout((0, 1))
    )
    spectra = whiten(projected).reshape(seg_dev, block_width, 2 * FREQS)
    own = jnp.transpose(spectra, (0, 2, 1)).reshape(spec_rows, block_width)
    owner_index = lax.axis_index("pairs")
    core = owner_index % 2
    chip = owner_index // 2
    first_core = core == 0
    z_index = lax.axis_index("z")
    y_index = lax.axis_index("y")
    gather_pos = jnp.where(first_core, y_index, z_index)
    reduce_pos = jnp.where(first_core, z_index, y_index)

    swap = [(p, p ^ 1) for p in range(pairs_count)]

    def chip_shift(d):
        return [(p, 2 * ((p // 2 + d) % chips) + p % 2) for p in range(pairs_count)]

    partner = lax.ppermute(own, "pairs", swap)
    from_below = lax.ppermute(own, "pairs", chip_shift(1))
    from_above = lax.ppermute(own, "pairs", chip_shift(-1))
    from_far = lax.ppermute(own, "pairs", chip_shift(2))
    mine = jnp.stack([own, from_above, from_far, from_below])
    theirs = lax.ppermute(mine[1:], "pairs", swap)
    theirs = jnp.concatenate([partner[None], theirs])
    table = jnp.where(
        first_core, jnp.stack([mine, theirs], axis=1), jnp.stack([theirs, mine], axis=1)
    ).reshape((pairs_count,) + own.shape)
    own_pairs = lax.dynamic_index_in_dim(pair_list, owner_index, 0, keepdims=False)
    live_slots = jnp.arange(slot_count, dtype=jnp.int32) < pair_count[owner_index]
    position = ((own_pairs // 2 - chip) % chips) * 2 + own_pairs % 2
    left = jnp.stack(
        [lax.dynamic_index_in_dim(table, position[k, 0], 0, keepdims=False) for k in range(slot_count)]
    )
    right = jnp.stack(
        [lax.dynamic_index_in_dim(table, position[k, 1], 0, keepdims=False) for k in range(slot_count)]
    )
    left_t = jnp.transpose(left, (0, 2, 1)).reshape((slot_count, side, side, rows, spec_rows))
    left_t = jnp.where(first_core, jnp.swapaxes(left_t, 1, 2), left_t)
    packed_rows = spec_rows * side * rows // block_width
    packs = jnp.transpose(left_t, (1, 0, 2, 3, 4)).reshape(
        (side, slot_count, packed_rows, block_width)
    )

    def rows_for(pos):
        return lax.dynamic_index_in_dim(packs, pos, 0, keepdims=False)

    def gather_perm(d):
        perm = []
        for p in range(pairs_count):
            for z in range(side):
                for y in range(side):
                    src = (p * side + z) * side + y
                    if p % 2 == 0:
                        dst = (p * side + z) * side + (y + d) % side
                    else:
                        dst = (p * side + (z + d) % side) * side + y
                    perm.append((src, dst))
        return perm

    def reduce_perm(e):
        perm = []
        for p in range(pairs_count):
            for z in range(side):
                for y in range(side):
                    src = (p * side + z) * side + y
                    if p % 2 == 0:
                        dst = (p * side + (z + e) % side) * side + y
                    else:
                        dst = (p * side + z) * side + (y + e) % side
                    perm.append((src, dst))
        return perm

    axes = ("pairs", "z", "y")
    pieces = [jnp.concatenate([right, rows_for(gather_pos)], axis=1)]
    for d in range(1, side):
        message = jnp.concatenate([right, rows_for((gather_pos + d) % side)], axis=1)
        pieces.append(lax.ppermute(message, axes, gather_perm(d)))
    gathered = jnp.stack(pieces)
    right_all = gathered[:, :, :spec_rows].reshape(
        (side, slot_count, seg_dev, 2, FREQS, block_width)
    )
    left_all = gathered[:, :, spec_rows:].reshape((side, slot_count, side * rows, seg_dev, 2, FREQS))
    left_all = jnp.transpose(left_all, (0, 1, 3, 4, 5, 2))
    right_swapped = jnp.stack([right_all[:, :, :, 1], -right_all[:, :, :, 0]], axis=3)
    rhs = jnp.concatenate([right_all, right_swapped], axis=-1)
    partial_value = jnp.einsum(
        "akscfm,akscfn->kfmn", left_all, rhs, preferred_element_type=jnp.float32
    )
    partial_value = partial_value.reshape((slot_count, FREQS, side, rows, 2, block_width))
    partial_value = jnp.transpose(partial_value, (2, 0, 4, 1, 3, 5)).astype(jnp.bfloat16)
    chunk_rows = slot_count * 2 * FREQS * rows
    partial_value = partial_value.reshape((side, chunk_rows, block_width))
    stacked = lax.dynamic_index_in_dim(partial_value, reduce_pos, 0, keepdims=False).astype(
        jnp.float32
    )
    for e in range(1, side):
        chunk = lax.dynamic_index_in_dim(partial_value, (reduce_pos + e) % side, 0, keepdims=False)
        stacked = stacked + lax.ppermute(chunk, axes, reduce_perm(e)).astype(jnp.float32)
    stacked = stacked.reshape((slot_count, 2, FREQS, rows, block_width))
    lag_weights = lag_table(seg_dev * side * side).reshape(2, FREQS, LAGS)
    correlation = jnp.einsum(
        "kpfrj,pft->krjt",
        stacked,
        lag_weights,
        precision=lax.Precision.DEFAULT,
        preferred_element_type=jnp.float32,
    )
    masked = correlation * live_slots.astype(jnp.float32)[:, None, None, None]
    return masked.astype(jnp.bfloat16)[None]


def solution(mesh):
    pairs_count, win_count = mesh.devices.shape
    side = math.isqrt(win_count)
    grid = Mesh(mesh.devices.reshape(pairs_count, side, side), ("pairs", "z", "y"))
    in_specs = (P("pairs", ("z", "y"), None, None), P(), P())
    out_specs = P("pairs", None, ("z", "y"), None, None)
    return jax.shard_map(shards, mesh=grid, in_specs=in_specs, out_specs=out_specs, check_vma=False)
```

```python
import math

import jax
import jax.numpy as jnp
import ml_dtypes
import numpy as np
from jax import lax
from jax.experimental.layout import Layout, with_layout_constraint
from jax.sharding import Mesh
from jax.sharding import PartitionSpec as P

NSAMP = 4096
FREQS = 32
LOW_BIN = 16
LAGS = 128


WATER = 0.1


def band_table():
    sample_idx = np.arange(NSAMP, dtype=np.int64)
    bin_idx = np.arange(FREQS, dtype=np.int64) + LOW_BIN
    phase = (sample_idx[:, None] * bin_idx[None, :] % NSAMP).astype(np.float64) * (
        2.0 * math.pi / NSAMP
    )
    scaled = np.concatenate([np.cos(phase), -np.sin(phase)], axis=1) * (1.0 / math.sqrt(NSAMP))
    return jnp.asarray(scaled.astype(ml_dtypes.bfloat16))


def lag_table(segments):
    bin_idx = jnp.arange(FREQS, dtype=jnp.int32) + LOW_BIN
    lag_idx = (jnp.arange(LAGS, dtype=jnp.int32) - LAGS // 2) * (NSAMP // LAGS)
    phase = (bin_idx[:, None] * lag_idx[None, :] % NSAMP).astype(jnp.float32) * (
        2.0 * math.pi / NSAMP
    )
    return jnp.concatenate([jnp.cos(phase), -jnp.sin(phase)], axis=0) * (
        1.0 / math.sqrt(segments * FREQS)
    )


def whiten(spectra):
    real_part = spectra[..., :FREQS]
    imag_part = spectra[..., FREQS:]
    power_bins = real_part * real_part + imag_part * imag_part
    widths = [(0, 0)] * (power_bins.ndim - 1) + [(2, 2)]
    padded = jnp.pad(power_bins, widths)
    smooth = (
        padded[..., 0:FREQS]
        + padded[..., 1 : FREQS + 1]
        + padded[..., 2 : FREQS + 2]
        + padded[..., 3 : FREQS + 3]
        + padded[..., 4 : FREQS + 4]
    ) * 0.2
    water_level = smooth + WATER * jnp.mean(power_bins, axis=-1, keepdims=True) + 1e-06
    factor = lax.rsqrt(water_level)
    return jnp.concatenate([real_part * factor, imag_part * factor], axis=-1).astype(jnp.bfloat16)


def shards(records, pair_list, pair_count):
    seg_dev = records.shape[1]
    block_width = records.shape[2]
    slot_count = pair_list.shape[1]
    pairs_count = lax.axis_size("pairs")
    side = lax.axis_size("y")
    rows = block_width // (side * side)
    chips = pairs_count // 2
    width = 2 * FREQS
    spec_rows = seg_dev * width
    half_rows = spec_rows // 2
    samples = records[0].reshape(seg_dev * block_width, NSAMP)
    projected = with_layout_constraint(
        jnp.dot(samples, band_table(), preferred_element_type=jnp.float32), Layout((0, 1))
    )
    spectra = whiten(projected).reshape(seg_dev, block_width, 2 * FREQS)
    own = jnp.transpose(spectra, (0, 2, 1)).reshape(spec_rows, block_width)
    owner_index = lax.axis_index("pairs")
    core = owner_index % 2
    chip = owner_index // 2
    first_core = core == 0
    z_index = lax.axis_index("z")
    y_index = lax.axis_index("y")
    gather_pos = jnp.where(first_core, y_index, z_index)
    reduce_pos = jnp.where(first_core, z_index, y_index)

    swap = [(p, p ^ 1) for p in range(pairs_count)]

    def chip_shift(d):
        return [(p, 2 * ((p // 2 + d) % chips) + p % 2) for p in range(pairs_count)]

    partner = lax.ppermute(own, "pairs", swap)
    from_below = lax.ppermute(own, "pairs", chip_shift(1))
    from_above = lax.ppermute(own, "pairs", chip_shift(-1))
    from_far = lax.ppermute(own, "pairs", chip_shift(2))
    mine = jnp.stack([own, from_above, from_far, from_below])
    theirs = lax.ppermute(mine[1:], "pairs", swap)
    theirs = jnp.concatenate([partner[None], theirs])
    table = jnp.where(
        first_core, jnp.stack([mine, theirs], axis=1), jnp.stack([theirs, mine], axis=1)
    ).reshape((pairs_count,) + own.shape)
    own_pairs = lax.dynamic_index_in_dim(pair_list, owner_index, 0, keepdims=False)
    live_slots = jnp.arange(slot_count, dtype=jnp.int32) < pair_count[owner_index]
    position = ((own_pairs // 2 - chip) % chips) * 2 + own_pairs % 2
    left = jnp.take(table, position[:, 0], axis=0)
    right = jnp.take(table, position[:, 1], axis=0)
    left_t = jnp.transpose(left, (0, 2, 1)).reshape((slot_count, side, side, rows, spec_rows))
    left_t = jnp.where(first_core, jnp.swapaxes(left_t, 1, 2), left_t)
    packed_rows = spec_rows * side * rows // block_width
    packs = jnp.transpose(left_t, (1, 0, 2, 3, 4)).reshape(
        (side, slot_count, packed_rows, block_width)
    )

    def rows_for(pos):
        return lax.dynamic_index_in_dim(packs, pos, 0, keepdims=False)

    def gather_perm(d):
        perm = []
        for p in range(pairs_count):
            for z in range(side):
                for y in range(side):
                    src = (p * side + z) * side + y
                    if p % 2 == 0:
                        dst = (p * side + z) * side + (y + d) % side
                    else:
                        dst = (p * side + (z + d) % side) * side + y
                    perm.append((src, dst))
        return perm

    def reduce_perm(e):
        perm = []
        for p in range(pairs_count):
            for z in range(side):
                for y in range(side):
                    src = (p * side + z) * side + y
                    if p % 2 == 0:
                        dst = (p * side + (z + e) % side) * side + y
                    else:
                        dst = (p * side + z) * side + (y + e) % side
                    perm.append((src, dst))
        return perm

    axes = ("pairs", "z", "y")
    pieces = [jnp.concatenate([right, rows_for(gather_pos)], axis=1)]
    for d in range(1, side):
        message = jnp.concatenate([right, rows_for((gather_pos + d) % side)], axis=1)
        pieces.append(lax.ppermute(message, axes, gather_perm(d)))
    gathered = jnp.stack(pieces)
    right_all = gathered[:, :, :spec_rows].reshape(
        (side, slot_count, seg_dev, 2, FREQS, block_width)
    )
    left_all = gathered[:, :, spec_rows:].reshape((side, slot_count, side * rows, seg_dev, 2, FREQS))
    left_all = jnp.transpose(left_all, (0, 1, 3, 4, 5, 2))
    right_swapped = jnp.stack([right_all[:, :, :, 1], -right_all[:, :, :, 0]], axis=3)
    rhs = jnp.concatenate([right_all, right_swapped], axis=-1)
    partial_value = jnp.einsum(
        "akscfm,akscfn->kfmn", left_all, rhs, preferred_element_type=jnp.float32
    )
    partial_value = partial_value.reshape((slot_count, FREQS, side, rows, 2, block_width))
    partial_value = jnp.transpose(partial_value, (2, 0, 4, 1, 3, 5)).astype(jnp.bfloat16)
    chunk_rows = slot_count * 2 * FREQS * rows
    partial_value = partial_value.reshape((side, chunk_rows, block_width))
    stacked = lax.dynamic_index_in_dim(partial_value, reduce_pos, 0, keepdims=False).astype(
        jnp.float32
    )
    for e in range(1, side):
        chunk = lax.dynamic_index_in_dim(partial_value, (reduce_pos + e) % side, 0, keepdims=False)
        stacked = stacked + lax.ppermute(chunk, axes, reduce_perm(e)).astype(jnp.float32)
    stacked = stacked.reshape((slot_count, 2, FREQS, rows, block_width))
    lag_weights = lag_table(seg_dev * side * side).reshape(2, FREQS, LAGS)
    correlation = jnp.einsum(
        "kpfrj,pft->krjt",
        stacked,
        lag_weights,
        precision=lax.Precision.DEFAULT,
        preferred_element_type=jnp.float32,
    )
    masked = correlation * live_slots.astype(jnp.float32)[:, None, None, None]
    return masked.astype(jnp.bfloat16)[None]


def solution(mesh):
    pairs_count, win_count = mesh.devices.shape
    side = math.isqrt(win_count)
    grid = Mesh(mesh.devices.reshape(pairs_count, side, side), ("pairs", "z", "y"))
    in_specs = (P("pairs", ("z", "y"), None, None), P(), P())
    out_specs = P("pairs", None, ("z", "y"), None, None)
    return jax.shard_map(shards, mesh=grid, in_specs=in_specs, out_specs=out_specs, check_vma=False)
```

```python
import math

import jax
import jax.numpy as jnp
import ml_dtypes
import numpy as np
from jax import lax
from jax.experimental.layout import Layout, with_layout_constraint
from jax.sharding import Mesh
from jax.sharding import PartitionSpec as P

NSAMP = 4096
FREQS = 32
LOW_BIN = 16
LAGS = 128


WATER = 0.1


def band_table():
    sample_idx = np.arange(NSAMP, dtype=np.int64)
    bin_idx = np.arange(FREQS, dtype=np.int64) + LOW_BIN
    phase = (sample_idx[:, None] * bin_idx[None, :] % NSAMP).astype(np.float64) * (
        2.0 * math.pi / NSAMP
    )
    scaled = np.concatenate([np.cos(phase), -np.sin(phase)], axis=1) * (1.0 / math.sqrt(NSAMP))
    return jnp.asarray(scaled.astype(ml_dtypes.bfloat16))


def lag_table(segments):
    bin_idx = jnp.arange(FREQS, dtype=jnp.int32) + LOW_BIN
    lag_idx = (jnp.arange(LAGS, dtype=jnp.int32) - LAGS // 2) * (NSAMP // LAGS)
    phase = (bin_idx[:, None] * lag_idx[None, :] % NSAMP).astype(jnp.float32) * (
        2.0 * math.pi / NSAMP
    )
    return jnp.concatenate([jnp.cos(phase), -jnp.sin(phase)], axis=0) * (
        1.0 / math.sqrt(segments * FREQS)
    )


def whiten(spectra):
    real_part = spectra[..., :FREQS]
    imag_part = spectra[..., FREQS:]
    power_bins = real_part * real_part + imag_part * imag_part
    widths = [(0, 0)] * (power_bins.ndim - 1) + [(2, 2)]
    padded = jnp.pad(power_bins, widths)
    smooth = (
        padded[..., 0:FREQS]
        + padded[..., 1 : FREQS + 1]
        + padded[..., 2 : FREQS + 2]
        + padded[..., 3 : FREQS + 3]
        + padded[..., 4 : FREQS + 4]
    ) * 0.2
    water_level = smooth + WATER * jnp.mean(power_bins, axis=-1, keepdims=True) + 1e-06
    factor = lax.rsqrt(water_level)
    return jnp.concatenate([real_part * factor, imag_part * factor], axis=-1).astype(jnp.bfloat16)


def shards(records, pair_list, pair_count):
    seg_dev = records.shape[1]
    block_width = records.shape[2]
    slot_count = pair_list.shape[1]
    pairs_count = lax.axis_size("pairs")
    side = lax.axis_size("y")
    rows = block_width // (side * side)
    chips = pairs_count // 2
    width = 2 * FREQS
    spec_rows = seg_dev * width
    half_rows = spec_rows // 2
    samples = records[0].reshape(seg_dev * block_width, NSAMP)
    projected = with_layout_constraint(
        jnp.dot(samples, band_table(), preferred_element_type=jnp.float32), Layout((0, 1))
    )
    spectra = whiten(projected).reshape(seg_dev, block_width, 2 * FREQS)
    own = jnp.transpose(spectra, (0, 2, 1)).reshape(spec_rows, block_width)
    owner_index = lax.axis_index("pairs")
    core = owner_index % 2
    chip = owner_index // 2
    first_core = core == 0
    z_index = lax.axis_index("z")
    y_index = lax.axis_index("y")
    gather_pos = jnp.where(first_core, y_index, z_index)
    reduce_pos = jnp.where(first_core, z_index, y_index)

    swap = [(p, p ^ 1) for p in range(pairs_count)]

    def chip_shift(d):
        return [(p, 2 * ((p // 2 + d) % chips) + p % 2) for p in range(pairs_count)]

    partner = lax.ppermute(own, "pairs", swap)
    from_below = lax.ppermute(own, "pairs", chip_shift(1))
    from_above = lax.ppermute(own, "pairs", chip_shift(-1))
    from_far = lax.ppermute(own, "pairs", chip_shift(2))
    mine = jnp.stack([own, from_above, from_far, from_below])
    theirs = lax.ppermute(mine[1:], "pairs", swap)
    theirs = jnp.concatenate([partner[None], theirs])
    table = jnp.where(
        first_core, jnp.stack([mine, theirs], axis=1), jnp.stack([theirs, mine], axis=1)
    ).reshape((pairs_count,) + own.shape)
    own_pairs = lax.dynamic_index_in_dim(pair_list, owner_index, 0, keepdims=False)
    live_slots = jnp.arange(slot_count, dtype=jnp.int32) < pair_count[owner_index]
    position = ((own_pairs // 2 - chip) % chips) * 2 + own_pairs % 2
    left = jnp.take(table, position[:, 0], axis=0)
    right = jnp.take(table, position[:, 1], axis=0)
    left_t = jnp.transpose(left, (0, 2, 1)).reshape((slot_count, side, side, rows, spec_rows))
    left_t = jnp.where(first_core, jnp.swapaxes(left_t, 1, 2), left_t)
    packed_rows = spec_rows * side * rows // block_width
    packs = jnp.transpose(left_t, (1, 0, 2, 3, 4)).reshape(
        (side, slot_count, packed_rows, block_width)
    )

    def rows_for(pos):
        return lax.dynamic_index_in_dim(packs, pos, 0, keepdims=False)

    def gather_perm(d):
        perm = []
        for p in range(pairs_count):
            for z in range(side):
                for y in range(side):
                    src = (p * side + z) * side + y
                    if p % 2 == 0:
                        dst = (p * side + z) * side + (y + d) % side
                    else:
                        dst = (p * side + (z + d) % side) * side + y
                    perm.append((src, dst))
        return perm

    def reduce_perm(e):
        perm = []
        for p in range(pairs_count):
            for z in range(side):
                for y in range(side):
                    src = (p * side + z) * side + y
                    if p % 2 == 0:
                        dst = (p * side + (z + e) % side) * side + y
                    else:
                        dst = (p * side + z) * side + (y + e) % side
                    perm.append((src, dst))
        return perm

    axes = ("pairs", "z", "y")
    pieces = [jnp.concatenate([right, rows_for(gather_pos)], axis=1)]
    for d in sorted(range(1, side), key=lambda step: -min(step, side - step)):
        message = jnp.concatenate([right, rows_for((gather_pos + d) % side)], axis=1)
        pieces.append(lax.ppermute(message, axes, gather_perm(d)))
    gathered = jnp.stack(pieces)
    right_all = gathered[:, :, :spec_rows].reshape(
        (side, slot_count, seg_dev, 2, FREQS, block_width)
    )
    left_all = gathered[:, :, spec_rows:].reshape((side, slot_count, side * rows, seg_dev, 2, FREQS))
    left_all = jnp.transpose(left_all, (0, 1, 3, 4, 5, 2))
    right_swapped = jnp.stack([right_all[:, :, :, 1], -right_all[:, :, :, 0]], axis=3)
    rhs = jnp.concatenate([right_all, right_swapped], axis=-1)
    partial_value = jnp.einsum(
        "akscfm,akscfn->kfmn", left_all, rhs, preferred_element_type=jnp.float32
    )
    partial_value = partial_value.reshape((slot_count, FREQS, side, rows, 2, block_width))
    partial_value = jnp.transpose(partial_value, (2, 0, 4, 1, 3, 5)).astype(jnp.bfloat16)
    chunk_rows = slot_count * 2 * FREQS * rows
    partial_value = partial_value.reshape((side, chunk_rows, block_width))
    stacked = lax.dynamic_index_in_dim(partial_value, reduce_pos, 0, keepdims=False).astype(
        jnp.float32
    )
    for e in sorted(range(1, side), key=lambda step: -min(step, side - step)):
        chunk = lax.dynamic_index_in_dim(partial_value, (reduce_pos + e) % side, 0, keepdims=False)
        stacked = stacked + lax.ppermute(chunk, axes, reduce_perm(e)).astype(jnp.float32)
    stacked = stacked.reshape((slot_count, 2, FREQS, rows, block_width))
    lag_weights = lag_table(seg_dev * side * side).reshape(2, FREQS, LAGS)
    correlation = jnp.einsum(
        "kpfrj,pft->krjt",
        stacked,
        lag_weights,
        precision=lax.Precision.DEFAULT,
        preferred_element_type=jnp.float32,
    )
    masked = correlation * live_slots.astype(jnp.float32)[:, None, None, None]
    return masked.astype(jnp.bfloat16)[None]


def solution(mesh):
    pairs_count, win_count = mesh.devices.shape
    side = math.isqrt(win_count)
    grid = Mesh(mesh.devices.reshape(pairs_count, side, side), ("pairs", "z", "y"))
    in_specs = (P("pairs", ("z", "y"), None, None), P(), P())
    out_specs = P("pairs", None, ("z", "y"), None, None)
    return jax.shard_map(shards, mesh=grid, in_specs=in_specs, out_specs=out_specs, check_vma=False)
```

```python
import math

import jax
import jax.numpy as jnp
import ml_dtypes
import numpy as np
from jax import lax
from jax.experimental.layout import Layout, with_layout_constraint
from jax.sharding import Mesh
from jax.sharding import PartitionSpec as P

NSAMP = 4096
FREQS = 32
LOW_BIN = 16
LAGS = 128


WATER = 0.1


def band_table():
    sample_idx = np.arange(NSAMP, dtype=np.int64)
    bin_idx = np.arange(FREQS, dtype=np.int64) + LOW_BIN
    phase = (sample_idx[:, None] * bin_idx[None, :] % NSAMP).astype(np.float64) * (
        2.0 * math.pi / NSAMP
    )
    scaled = np.concatenate([np.cos(phase), -np.sin(phase)], axis=1) * (1.0 / math.sqrt(NSAMP))
    return jnp.asarray(scaled.astype(ml_dtypes.bfloat16))


def lag_table(segments):
    bin_idx = jnp.arange(FREQS, dtype=jnp.int32) + LOW_BIN
    lag_idx = (jnp.arange(LAGS, dtype=jnp.int32) - LAGS // 2) * (NSAMP // LAGS)
    phase = (bin_idx[:, None] * lag_idx[None, :] % NSAMP).astype(jnp.float32) * (
        2.0 * math.pi / NSAMP
    )
    return jnp.concatenate([jnp.cos(phase), -jnp.sin(phase)], axis=0) * (
        1.0 / math.sqrt(segments * FREQS)
    )


def whiten(spectra):
    real_part = spectra[..., :FREQS]
    imag_part = spectra[..., FREQS:]
    power_bins = real_part * real_part + imag_part * imag_part
    widths = [(0, 0)] * (power_bins.ndim - 1) + [(2, 2)]
    padded = jnp.pad(power_bins, widths)
    smooth = (
        padded[..., 0:FREQS]
        + padded[..., 1 : FREQS + 1]
        + padded[..., 2 : FREQS + 2]
        + padded[..., 3 : FREQS + 3]
        + padded[..., 4 : FREQS + 4]
    ) * 0.2
    water_level = smooth + WATER * jnp.mean(power_bins, axis=-1, keepdims=True) + 1e-06
    factor = lax.rsqrt(water_level)
    return jnp.concatenate([real_part * factor, imag_part * factor], axis=-1).astype(jnp.bfloat16)


def shards(records, pair_list, pair_count):
    seg_dev = records.shape[1]
    block_width = records.shape[2]
    slot_count = pair_list.shape[1]
    pairs_count = lax.axis_size("pairs")
    side = lax.axis_size("y")
    rows = block_width // (side * side)
    chips = pairs_count // 2
    width = 2 * FREQS
    spec_rows = seg_dev * width
    half_rows = spec_rows // 2
    samples = records[0].reshape(seg_dev * block_width, NSAMP)
    projected = with_layout_constraint(
        jnp.dot(samples, band_table(), preferred_element_type=jnp.float32), Layout((0, 1))
    )
    spectra = whiten(projected).reshape(seg_dev, block_width, 2 * FREQS)
    own = jnp.transpose(spectra, (0, 2, 1)).reshape(spec_rows, block_width)
    owner_index = lax.axis_index("pairs")
    core = owner_index % 2
    chip = owner_index // 2
    first_core = core == 0
    z_index = lax.axis_index("z")
    y_index = lax.axis_index("y")
    gather_pos = jnp.where(first_core, y_index, z_index)
    reduce_pos = jnp.where(first_core, z_index, y_index)

    swap = [(p, p ^ 1) for p in range(pairs_count)]

    def chip_shift(d):
        return [(p, 2 * ((p // 2 + d) % chips) + p % 2) for p in range(pairs_count)]

    partner = lax.ppermute(own, "pairs", swap)
    from_below = lax.ppermute(own, "pairs", chip_shift(1))
    from_above = lax.ppermute(own, "pairs", chip_shift(-1))
    from_far = lax.ppermute(own, "pairs", chip_shift(2))
    mine = jnp.stack([own, from_above, from_far, from_below])
    theirs = lax.ppermute(mine[1:], "pairs", swap)
    theirs = jnp.concatenate([partner[None], theirs])
    table = jnp.where(
        first_core, jnp.stack([mine, theirs], axis=1), jnp.stack([theirs, mine], axis=1)
    ).reshape((pairs_count,) + own.shape)
    own_pairs = lax.dynamic_index_in_dim(pair_list, owner_index, 0, keepdims=False)
    live_slots = jnp.arange(slot_count, dtype=jnp.int32) < pair_count[owner_index]
    position = ((own_pairs // 2 - chip) % chips) * 2 + own_pairs % 2
    left = jnp.take(table, position[:, 0], axis=0)
    right = jnp.take(table, position[:, 1], axis=0)
    left_t = jnp.transpose(left, (0, 2, 1)).reshape((slot_count, side, side, rows, spec_rows))
    left_t = jnp.where(first_core, jnp.swapaxes(left_t, 1, 2), left_t)
    packed_rows = spec_rows * side * rows // block_width
    packs = jnp.transpose(left_t, (1, 0, 2, 3, 4)).reshape(
        (side, slot_count, packed_rows, block_width)
    )

    def rows_for(pos):
        return lax.dynamic_index_in_dim(packs, pos, 0, keepdims=False)

    def gather_perm(d):
        perm = []
        for p in range(pairs_count):
            for z in range(side):
                for y in range(side):
                    src = (p * side + z) * side + y
                    if p % 2 == 0:
                        dst = (p * side + z) * side + (y + d) % side
                    else:
                        dst = (p * side + (z + d) % side) * side + y
                    perm.append((src, dst))
        return perm

    def reduce_perm(e):
        perm = []
        for p in range(pairs_count):
            for z in range(side):
                for y in range(side):
                    src = (p * side + z) * side + y
                    if p % 2 == 0:
                        dst = (p * side + (z + e) % side) * side + y
                    else:
                        dst = (p * side + z) * side + (y + e) % side
                    perm.append((src, dst))
        return perm

    axes = ("pairs", "z", "y")
    pieces = [jnp.concatenate([right, rows_for(gather_pos)], axis=1)]
    for d in sorted(range(1, side), key=lambda step: -min(step, side - step)):
        message = jnp.concatenate([right, rows_for((gather_pos + d) % side)], axis=1)
        pieces.append(lax.ppermute(message, axes, gather_perm(d)))
    left_pieces = []
    right_pieces = []
    for piece in pieces:
        left_piece = piece[:, spec_rows:].reshape((slot_count, side * rows, seg_dev, 2, FREQS))
        left_pieces.append(jnp.transpose(left_piece, (0, 4, 3, 2, 1)))
        right_piece = piece[:, :spec_rows].reshape((slot_count, seg_dev, 2, FREQS, block_width))
        right_pieces.append(jnp.transpose(right_piece, (0, 3, 2, 1, 4)))
    left_all = jnp.stack(left_pieces, axis=2)
    right_all = jnp.stack(right_pieces, axis=2)
    right_swapped = jnp.stack([right_all[:, :, :, 1], -right_all[:, :, :, 0]], axis=3)
    rhs = jnp.concatenate([right_all, right_swapped], axis=-1)
    partial_value = jnp.einsum(
        "kfacsm,kfacsn->kfmn", left_all, rhs, preferred_element_type=jnp.float32
    )
    partial_value = partial_value.reshape((slot_count, FREQS, side, rows, 2, block_width))
    partial_value = jnp.transpose(partial_value, (2, 0, 4, 1, 3, 5)).astype(jnp.bfloat16)
    chunk_rows = slot_count * 2 * FREQS * rows
    partial_value = partial_value.reshape((side, chunk_rows, block_width))
    stacked = lax.dynamic_index_in_dim(partial_value, reduce_pos, 0, keepdims=False).astype(
        jnp.float32
    )
    for e in sorted(range(1, side), key=lambda step: -min(step, side - step)):
        chunk = lax.dynamic_index_in_dim(partial_value, (reduce_pos + e) % side, 0, keepdims=False)
        stacked = stacked + lax.ppermute(chunk, axes, reduce_perm(e)).astype(jnp.float32)
    stacked = stacked.reshape((slot_count, 2, FREQS, rows, block_width))
    lag_weights = lag_table(seg_dev * side * side).reshape(2, FREQS, LAGS)
    correlation = jnp.einsum(
        "kpfrj,pft->krjt",
        stacked,
        lag_weights,
        precision=lax.Precision.DEFAULT,
        preferred_element_type=jnp.float32,
    )
    masked = correlation * live_slots.astype(jnp.float32)[:, None, None, None]
    return masked.astype(jnp.bfloat16)[None]


def solution(mesh):
    pairs_count, win_count = mesh.devices.shape
    side = math.isqrt(win_count)
    grid = Mesh(mesh.devices.reshape(pairs_count, side, side), ("pairs", "z", "y"))
    in_specs = (P("pairs", ("z", "y"), None, None), P(), P())
    out_specs = P("pairs", None, ("z", "y"), None, None)
    return jax.shard_map(shards, mesh=grid, in_specs=in_specs, out_specs=out_specs, check_vma=False)
```

```python
import math

import jax
import jax.numpy as jnp
import ml_dtypes
import numpy as np
from jax import lax
from jax.experimental.layout import Layout, with_layout_constraint
from jax.sharding import Mesh
from jax.sharding import PartitionSpec as P

NSAMP = 4096
FREQS = 32
LOW_BIN = 16
LAGS = 128


WATER = 0.1


def band_table():
    sample_idx = np.arange(NSAMP, dtype=np.int64)
    bin_idx = np.arange(FREQS, dtype=np.int64) + LOW_BIN
    phase = (sample_idx[:, None] * bin_idx[None, :] % NSAMP).astype(np.float64) * (
        2.0 * math.pi / NSAMP
    )
    scaled = np.concatenate([np.cos(phase), -np.sin(phase)], axis=1) * (1.0 / math.sqrt(NSAMP))
    return jnp.asarray(scaled.astype(ml_dtypes.bfloat16))


def lag_table(segments):
    bin_idx = jnp.arange(FREQS, dtype=jnp.int32) + LOW_BIN
    lag_idx = (jnp.arange(LAGS, dtype=jnp.int32) - LAGS // 2) * (NSAMP // LAGS)
    phase = (bin_idx[:, None] * lag_idx[None, :] % NSAMP).astype(jnp.float32) * (
        2.0 * math.pi / NSAMP
    )
    return jnp.concatenate([jnp.cos(phase), -jnp.sin(phase)], axis=0) * (
        1.0 / math.sqrt(segments * FREQS)
    )


def whiten(spectra):
    real_part = spectra[..., :FREQS]
    imag_part = spectra[..., FREQS:]
    power_bins = real_part * real_part + imag_part * imag_part
    widths = [(0, 0)] * (power_bins.ndim - 1) + [(2, 2)]
    padded = jnp.pad(power_bins, widths)
    smooth = (
        padded[..., 0:FREQS]
        + padded[..., 1 : FREQS + 1]
        + padded[..., 2 : FREQS + 2]
        + padded[..., 3 : FREQS + 3]
        + padded[..., 4 : FREQS + 4]
    ) * 0.2
    water_level = smooth + WATER * jnp.mean(power_bins, axis=-1, keepdims=True) + 1e-06
    factor = lax.rsqrt(water_level)
    return jnp.concatenate([real_part * factor, imag_part * factor], axis=-1).astype(jnp.bfloat16)


def shards(records, pair_list, pair_count):
    seg_dev = records.shape[1]
    block_width = records.shape[2]
    slot_count = pair_list.shape[1]
    pairs_count = lax.axis_size("pairs")
    side = lax.axis_size("y")
    rows = block_width // (side * side)
    chips = pairs_count // 2
    width = 2 * FREQS
    spec_rows = seg_dev * width
    half_rows = spec_rows // 2
    samples = records[0].reshape(seg_dev * block_width, NSAMP)
    projected = with_layout_constraint(
        jnp.dot(samples, band_table(), preferred_element_type=jnp.float32), Layout((0, 1))
    )
    spectra = whiten(projected).reshape(seg_dev, block_width, 2 * FREQS)
    own = jnp.transpose(spectra, (0, 2, 1)).reshape(spec_rows, block_width)
    owner_index = lax.axis_index("pairs")
    core = owner_index % 2
    chip = owner_index // 2
    first_core = core == 0
    z_index = lax.axis_index("z")
    y_index = lax.axis_index("y")
    gather_pos = jnp.where(first_core, y_index, z_index)
    reduce_pos = jnp.where(first_core, z_index, y_index)

    swap = [(p, p ^ 1) for p in range(pairs_count)]

    def chip_shift(d):
        return [(p, 2 * ((p // 2 + d) % chips) + p % 2) for p in range(pairs_count)]

    partner = lax.ppermute(own, "pairs", swap)
    from_below = lax.ppermute(own, "pairs", chip_shift(1))
    from_above = lax.ppermute(own, "pairs", chip_shift(-1))
    from_far = lax.ppermute(own, "pairs", chip_shift(2))
    mine = jnp.stack([own, from_above, from_far, from_below])
    theirs = lax.ppermute(mine[1:], "pairs", swap)
    theirs = jnp.concatenate([partner[None], theirs])
    table = jnp.where(
        first_core, jnp.stack([mine, theirs], axis=1), jnp.stack([theirs, mine], axis=1)
    ).reshape((pairs_count,) + own.shape)
    own_pairs = lax.dynamic_index_in_dim(pair_list, owner_index, 0, keepdims=False)
    live_slots = jnp.arange(slot_count, dtype=jnp.int32) < pair_count[owner_index]
    position = ((own_pairs // 2 - chip) % chips) * 2 + own_pairs % 2
    chosen = jnp.take(table, position.T.reshape(-1), axis=0)
    left = chosen[:slot_count]
    right = chosen[slot_count:]
    left_t = jnp.transpose(left, (0, 2, 1)).reshape((slot_count, side, side, rows, spec_rows))
    left_t = jnp.where(first_core, jnp.swapaxes(left_t, 1, 2), left_t)
    packed_rows = spec_rows * side * rows // block_width
    packs = jnp.transpose(left_t, (1, 0, 2, 3, 4)).reshape(
        (side, slot_count, packed_rows, block_width)
    )

    def rows_for(pos):
        return lax.dynamic_index_in_dim(packs, pos, 0, keepdims=False)

    def gather_perm(d):
        perm = []
        for p in range(pairs_count):
            for z in range(side):
                for y in range(side):
                    src = (p * side + z) * side + y
                    if p % 2 == 0:
                        dst = (p * side + z) * side + (y + d) % side
                    else:
                        dst = (p * side + (z + d) % side) * side + y
                    perm.append((src, dst))
        return perm

    def reduce_perm(e):
        perm = []
        for p in range(pairs_count):
            for z in range(side):
                for y in range(side):
                    src = (p * side + z) * side + y
                    if p % 2 == 0:
                        dst = (p * side + (z + e) % side) * side + y
                    else:
                        dst = (p * side + z) * side + (y + e) % side
                    perm.append((src, dst))
        return perm

    axes = ("pairs", "z", "y")
    pieces = [jnp.concatenate([right, rows_for(gather_pos)], axis=1)]
    for d in sorted(range(1, side), key=lambda step: -min(step, side - step)):
        message = jnp.concatenate([right, rows_for((gather_pos + d) % side)], axis=1)
        pieces.append(lax.ppermute(message, axes, gather_perm(d)))
    gathered = jnp.stack(pieces)
    right_all = gathered[:, :, :spec_rows].reshape(
        (side, slot_count, seg_dev, 2, FREQS, block_width)
    )
    left_all = gathered[:, :, spec_rows:].reshape((side, slot_count, side * rows, seg_dev, 2, FREQS))
    left_all = jnp.transpose(left_all, (0, 1, 3, 4, 5, 2))
    right_swapped = jnp.stack([right_all[:, :, :, 1], -right_all[:, :, :, 0]], axis=3)
    rhs = jnp.concatenate([right_all, right_swapped], axis=-1)
    partial_value = jnp.einsum(
        "akscfm,akscfn->kfmn", left_all, rhs, preferred_element_type=jnp.float32
    )
    partial_value = partial_value.reshape((slot_count, FREQS, side, rows, 2, block_width))
    partial_value = jnp.transpose(partial_value, (2, 0, 4, 1, 3, 5)).astype(jnp.bfloat16)
    chunk_rows = slot_count * 2 * FREQS * rows
    partial_value = partial_value.reshape((side, chunk_rows, block_width))
    stacked = lax.dynamic_index_in_dim(partial_value, reduce_pos, 0, keepdims=False).astype(
        jnp.float32
    )
    for e in sorted(range(1, side), key=lambda step: -min(step, side - step)):
        chunk = lax.dynamic_index_in_dim(partial_value, (reduce_pos + e) % side, 0, keepdims=False)
        stacked = stacked + lax.ppermute(chunk, axes, reduce_perm(e)).astype(jnp.float32)
    stacked = stacked.reshape((slot_count, 2, FREQS, rows, block_width))
    lag_weights = lag_table(seg_dev * side * side).reshape(2, FREQS, LAGS)
    correlation = jnp.einsum(
        "kpfrj,pft->krjt",
        stacked,
        lag_weights,
        precision=lax.Precision.DEFAULT,
        preferred_element_type=jnp.float32,
    )
    masked = correlation * live_slots.astype(jnp.float32)[:, None, None, None]
    return masked.astype(jnp.bfloat16)[None]


def solution(mesh):
    pairs_count, win_count = mesh.devices.shape
    side = math.isqrt(win_count)
    grid = Mesh(mesh.devices.reshape(pairs_count, side, side), ("pairs", "z", "y"))
    in_specs = (P("pairs", ("z", "y"), None, None), P(), P())
    out_specs = P("pairs", None, ("z", "y"), None, None)
    return jax.shard_map(shards, mesh=grid, in_specs=in_specs, out_specs=out_specs, check_vma=False)
```

```python
import math

import jax
import jax.numpy as jnp
import ml_dtypes
import numpy as np
from jax import lax
from jax.experimental.layout import Layout, with_layout_constraint
from jax.sharding import Mesh
from jax.sharding import PartitionSpec as P

NSAMP = 4096
FREQS = 32
LOW_BIN = 16
LAGS = 128


WATER = 0.1


def band_table():
    sample_idx = np.arange(NSAMP, dtype=np.int64)
    bin_idx = np.arange(FREQS, dtype=np.int64) + LOW_BIN
    phase = (sample_idx[:, None] * bin_idx[None, :] % NSAMP).astype(np.float64) * (
        2.0 * math.pi / NSAMP
    )
    scaled = np.concatenate([np.cos(phase), -np.sin(phase)], axis=1) * (1.0 / math.sqrt(NSAMP))
    return jnp.asarray(scaled.astype(ml_dtypes.bfloat16))


def lag_table(segments):
    bin_idx = jnp.arange(FREQS, dtype=jnp.int32) + LOW_BIN
    lag_idx = (jnp.arange(LAGS, dtype=jnp.int32) - LAGS // 2) * (NSAMP // LAGS)
    phase = (bin_idx[:, None] * lag_idx[None, :] % NSAMP).astype(jnp.float32) * (
        2.0 * math.pi / NSAMP
    )
    return jnp.concatenate([jnp.cos(phase), -jnp.sin(phase)], axis=0) * (
        1.0 / math.sqrt(segments * FREQS)
    )


def whiten(spectra):
    real_part = spectra[..., :FREQS]
    imag_part = spectra[..., FREQS:]
    power_bins = real_part * real_part + imag_part * imag_part
    widths = [(0, 0)] * (power_bins.ndim - 1) + [(2, 2)]
    padded = jnp.pad(power_bins, widths)
    smooth = (
        padded[..., 0:FREQS]
        + padded[..., 1 : FREQS + 1]
        + padded[..., 2 : FREQS + 2]
        + padded[..., 3 : FREQS + 3]
        + padded[..., 4 : FREQS + 4]
    ) * 0.2
    water_level = smooth + WATER * jnp.mean(power_bins, axis=-1, keepdims=True) + 1e-06
    factor = lax.rsqrt(water_level)
    return jnp.concatenate([real_part * factor, imag_part * factor], axis=-1).astype(jnp.bfloat16)


def shards(records, pair_list, pair_count):
    seg_dev = records.shape[1]
    block_width = records.shape[2]
    slot_count = pair_list.shape[1]
    pairs_count = lax.axis_size("pairs")
    side = lax.axis_size("y")
    rows = block_width // (side * side)
    chips = pairs_count // 2
    width = 2 * FREQS
    spec_rows = seg_dev * width
    half_rows = spec_rows // 2
    samples = records[0].reshape(seg_dev * block_width, NSAMP)
    projected = with_layout_constraint(
        jnp.dot(samples, band_table(), preferred_element_type=jnp.float32), Layout((0, 1))
    )
    spectra = whiten(projected).reshape(seg_dev, block_width, 2 * FREQS)
    own = jnp.transpose(spectra, (0, 2, 1)).reshape(spec_rows, block_width)
    owner_index = lax.axis_index("pairs")
    core = owner_index % 2
    chip = owner_index // 2
    first_core = core == 0
    z_index = lax.axis_index("z")
    y_index = lax.axis_index("y")
    gather_pos = jnp.where(first_core, y_index, z_index)
    reduce_pos = jnp.where(first_core, z_index, y_index)

    swap = [(p, p ^ 1) for p in range(pairs_count)]

    def chip_shift(d):
        return [(p, 2 * ((p // 2 + d) % chips) + p % 2) for p in range(pairs_count)]

    partner = lax.ppermute(own, "pairs", swap)
    from_below = lax.ppermute(own, "pairs", chip_shift(1))
    from_above = lax.ppermute(own, "pairs", chip_shift(-1))
    from_far = lax.ppermute(own, "pairs", chip_shift(2))
    mine = jnp.stack([own, from_above, from_far, from_below])
    theirs = lax.ppermute(mine[1:], "pairs", swap)
    theirs = jnp.concatenate([partner[None], theirs])
    table = jnp.concatenate([mine, theirs])
    own_pairs = lax.dynamic_index_in_dim(pair_list, owner_index, 0, keepdims=False)
    live_slots = jnp.arange(slot_count, dtype=jnp.int32) < pair_count[owner_index]
    position = (own_pairs // 2 - chip) % chips + chips * (own_pairs % 2 != core)
    chosen = jnp.take(table, position.T.reshape(-1), axis=0, mode="clip")
    left = chosen[:slot_count]
    right = chosen[slot_count:]
    left_t = jnp.transpose(left, (0, 2, 1)).reshape((slot_count, side, side, rows, spec_rows))
    left_t = jnp.where(first_core, jnp.swapaxes(left_t, 1, 2), left_t)
    packed_rows = spec_rows * side * rows // block_width
    packs = jnp.transpose(left_t, (1, 0, 2, 3, 4)).reshape(
        (side, slot_count, packed_rows, block_width)
    )

    def rows_for(pos):
        return lax.dynamic_index_in_dim(packs, pos, 0, keepdims=False)

    def gather_perm(d):
        perm = []
        for p in range(pairs_count):
            for z in range(side):
                for y in range(side):
                    src = (p * side + z) * side + y
                    if p % 2 == 0:
                        dst = (p * side + z) * side + (y + d) % side
                    else:
                        dst = (p * side + (z + d) % side) * side + y
                    perm.append((src, dst))
        return perm

    def reduce_perm(e):
        perm = []
        for p in range(pairs_count):
            for z in range(side):
                for y in range(side):
                    src = (p * side + z) * side + y
                    if p % 2 == 0:
                        dst = (p * side + (z + e) % side) * side + y
                    else:
                        dst = (p * side + z) * side + (y + e) % side
                    perm.append((src, dst))
        return perm

    axes = ("pairs", "z", "y")
    pieces = [jnp.concatenate([right, rows_for(gather_pos)], axis=1)]
    for d in sorted(range(1, side), key=lambda step: -min(step, side - step)):
        message = jnp.concatenate([right, rows_for((gather_pos + d) % side)], axis=1)
        pieces.append(lax.ppermute(message, axes, gather_perm(d)))
    gathered = jnp.stack(pieces)
    right_all = gathered[:, :, :spec_rows].reshape(
        (side, slot_count, seg_dev, 2, FREQS, block_width)
    )
    left_all = gathered[:, :, spec_rows:].reshape((side, slot_count, side * rows, seg_dev, 2, FREQS))
    left_all = jnp.transpose(left_all, (0, 1, 3, 4, 5, 2))
    right_swapped = jnp.stack([right_all[:, :, :, 1], -right_all[:, :, :, 0]], axis=3)
    rhs = jnp.concatenate([right_all, right_swapped], axis=-1)
    partial_value = jnp.einsum(
        "akscfm,akscfn->kfmn", left_all, rhs, preferred_element_type=jnp.float32
    )
    partial_value = partial_value.reshape((slot_count, FREQS, side, rows, 2, block_width))
    partial_value = jnp.transpose(partial_value, (2, 0, 4, 1, 3, 5)).astype(jnp.bfloat16)
    chunk_rows = slot_count * 2 * FREQS * rows
    partial_value = partial_value.reshape((side, chunk_rows, block_width))
    stacked = lax.dynamic_index_in_dim(partial_value, reduce_pos, 0, keepdims=False).astype(
        jnp.float32
    )
    for e in sorted(range(1, side), key=lambda step: -min(step, side - step)):
        chunk = lax.dynamic_index_in_dim(partial_value, (reduce_pos + e) % side, 0, keepdims=False)
        stacked = stacked + lax.ppermute(chunk, axes, reduce_perm(e)).astype(jnp.float32)
    stacked = stacked.reshape((slot_count, 2, FREQS, rows, block_width))
    lag_weights = lag_table(seg_dev * side * side).reshape(2, FREQS, LAGS)
    correlation = jnp.einsum(
        "kpfrj,pft->krjt",
        stacked,
        lag_weights,
        precision=lax.Precision.DEFAULT,
        preferred_element_type=jnp.float32,
    )
    masked = correlation * live_slots.astype(jnp.float32)[:, None, None, None]
    return masked.astype(jnp.bfloat16)[None]


def solution(mesh):
    pairs_count, win_count = mesh.devices.shape
    side = math.isqrt(win_count)
    grid = Mesh(mesh.devices.reshape(pairs_count, side, side), ("pairs", "z", "y"))
    in_specs = (P("pairs", ("z", "y"), None, None), P(), P())
    out_specs = P("pairs", None, ("z", "y"), None, None)
    return jax.shard_map(shards, mesh=grid, in_specs=in_specs, out_specs=out_specs, check_vma=False)
```

```python
import math

import jax
import jax.numpy as jnp
import ml_dtypes
import numpy as np
from jax import lax
from jax.sharding import Mesh
from jax.sharding import PartitionSpec as P

NSAMP = 4096
FREQS = 32
LOW_BIN = 16
LAGS = 128


WATER = 0.1


def band_table():
    sample_idx = np.arange(NSAMP, dtype=np.int64)
    bin_idx = np.arange(FREQS, dtype=np.int64) + LOW_BIN
    phase = (sample_idx[:, None] * bin_idx[None, :] % NSAMP).astype(np.float64) * (
        2.0 * math.pi / NSAMP
    )
    scaled = np.concatenate([np.cos(phase), -np.sin(phase)], axis=1) * (1.0 / math.sqrt(NSAMP))
    return jnp.asarray(scaled.astype(ml_dtypes.bfloat16))


def lag_table(segments):
    bin_idx = jnp.arange(FREQS, dtype=jnp.int32) + LOW_BIN
    lag_idx = (jnp.arange(LAGS, dtype=jnp.int32) - LAGS // 2) * (NSAMP // LAGS)
    phase = (bin_idx[:, None] * lag_idx[None, :] % NSAMP).astype(jnp.float32) * (
        2.0 * math.pi / NSAMP
    )
    return jnp.concatenate([jnp.cos(phase), -jnp.sin(phase)], axis=0) * (
        1.0 / math.sqrt(segments * FREQS)
    )


def whiten(spectra):
    real_part = spectra[..., :FREQS]
    imag_part = spectra[..., FREQS:]
    power_bins = real_part * real_part + imag_part * imag_part
    widths = [(0, 0)] * (power_bins.ndim - 1) + [(2, 2)]
    padded = jnp.pad(power_bins, widths)
    smooth = (
        padded[..., 0:FREQS]
        + padded[..., 1 : FREQS + 1]
        + padded[..., 2 : FREQS + 2]
        + padded[..., 3 : FREQS + 3]
        + padded[..., 4 : FREQS + 4]
    ) * 0.2
    water_level = smooth + WATER * jnp.mean(power_bins, axis=-1, keepdims=True) + 1e-06
    factor = lax.rsqrt(water_level)
    return jnp.concatenate([real_part * factor, imag_part * factor], axis=-1).astype(jnp.bfloat16)


def shards(records, pair_list, pair_count):
    seg_dev = records.shape[1]
    block_width = records.shape[2]
    slot_count = pair_list.shape[1]
    pairs_count = lax.axis_size("pairs")
    side = lax.axis_size("y")
    rows = block_width // (side * side)
    chips = pairs_count // 2
    width = 2 * FREQS
    spec_rows = seg_dev * width
    half_rows = spec_rows // 2
    spectra = whiten(jnp.dot(records[0], band_table(), preferred_element_type=jnp.float32))
    own = jnp.transpose(spectra, (0, 2, 1)).reshape(spec_rows, block_width)
    owner_index = lax.axis_index("pairs")
    core = owner_index % 2
    chip = owner_index // 2
    first_core = core == 0
    z_index = lax.axis_index("z")
    y_index = lax.axis_index("y")
    gather_pos = jnp.where(first_core, y_index, z_index)
    reduce_pos = jnp.where(first_core, z_index, y_index)

    swap = [(p, p ^ 1) for p in range(pairs_count)]

    def chip_shift(d):
        return [(p, 2 * ((p // 2 + d) % chips) + p % 2) for p in range(pairs_count)]

    partner = lax.ppermute(own, "pairs", swap)
    from_below = lax.ppermute(own, "pairs", chip_shift(1))
    from_above = lax.ppermute(own, "pairs", chip_shift(-1))
    from_far = lax.ppermute(own, "pairs", chip_shift(2))
    mine = jnp.stack([own, from_above, from_far, from_below])
    theirs = lax.ppermute(mine[1:], "pairs", swap)
    theirs = jnp.concatenate([partner[None], theirs])
    table = jnp.where(
        first_core, jnp.stack([mine, theirs], axis=1), jnp.stack([theirs, mine], axis=1)
    ).reshape((pairs_count,) + own.shape)
    own_pairs = lax.dynamic_index_in_dim(pair_list, owner_index, 0, keepdims=False)
    live_slots = jnp.arange(slot_count, dtype=jnp.int32) < pair_count[owner_index]
    position = ((own_pairs // 2 - chip) % chips) * 2 + own_pairs % 2
    chosen = jnp.take(table, position.T.reshape(-1), axis=0)
    left = chosen[:slot_count]
    right = chosen[slot_count:]
    left_t = jnp.transpose(left, (0, 2, 1)).reshape((slot_count, side, side, rows, spec_rows))
    left_t = jnp.where(first_core, jnp.swapaxes(left_t, 1, 2), left_t)
    packed_rows = spec_rows * side * rows // block_width
    packs = jnp.transpose(left_t, (1, 0, 2, 3, 4)).reshape(
        (side, slot_count, packed_rows, block_width)
    )

    def rows_for(pos):
        return lax.dynamic_index_in_dim(packs, pos, 0, keepdims=False)

    def gather_perm(d):
        perm = []
        for p in range(pairs_count):
            for z in range(side):
                for y in range(side):
                    src = (p * side + z) * side + y
                    if p % 2 == 0:
                        dst = (p * side + z) * side + (y + d) % side
                    else:
                        dst = (p * side + (z + d) % side) * side + y
                    perm.append((src, dst))
        return perm

    def reduce_perm(e):
        perm = []
        for p in range(pairs_count):
            for z in range(side):
                for y in range(side):
                    src = (p * side + z) * side + y
                    if p % 2 == 0:
                        dst = (p * side + (z + e) % side) * side + y
                    else:
                        dst = (p * side + z) * side + (y + e) % side
                    perm.append((src, dst))
        return perm

    axes = ("pairs", "z", "y")
    pieces = [jnp.concatenate([right, rows_for(gather_pos)], axis=1)]
    for d in sorted(range(1, side), key=lambda step: -min(step, side - step)):
        message = jnp.concatenate([right, rows_for((gather_pos + d) % side)], axis=1)
        pieces.append(lax.ppermute(message, axes, gather_perm(d)))
    gathered = jnp.stack(pieces)
    right_all = gathered[:, :, :spec_rows].reshape(
        (side, slot_count, seg_dev, 2, FREQS, block_width)
    )
    left_all = gathered[:, :, spec_rows:].reshape((side, slot_count, side * rows, seg_dev, 2, FREQS))
    left_all = jnp.transpose(left_all, (0, 1, 3, 4, 5, 2))
    right_swapped = jnp.stack([right_all[:, :, :, 1], -right_all[:, :, :, 0]], axis=3)
    rhs = jnp.concatenate([right_all, right_swapped], axis=-1)
    partial_value = jnp.einsum(
        "akscfm,akscfn->kfmn", left_all, rhs, preferred_element_type=jnp.float32
    )
    partial_value = partial_value.reshape((slot_count, FREQS, side, rows, 2, block_width))
    partial_value = jnp.transpose(partial_value, (2, 0, 4, 1, 3, 5)).astype(jnp.bfloat16)
    chunk_rows = slot_count * 2 * FREQS * rows
    partial_value = partial_value.reshape((side, chunk_rows, block_width))
    stacked = lax.dynamic_index_in_dim(partial_value, reduce_pos, 0, keepdims=False).astype(
        jnp.float32
    )
    for e in sorted(range(1, side), key=lambda step: -min(step, side - step)):
        chunk = lax.dynamic_index_in_dim(partial_value, (reduce_pos + e) % side, 0, keepdims=False)
        stacked = stacked + lax.ppermute(chunk, axes, reduce_perm(e)).astype(jnp.float32)
    stacked = stacked.reshape((slot_count, 2, FREQS, rows, block_width))
    lag_weights = lag_table(seg_dev * side * side).reshape(2, FREQS, LAGS)
    correlation = jnp.einsum(
        "kpfrj,pft->krjt",
        stacked,
        lag_weights,
        precision=lax.Precision.DEFAULT,
        preferred_element_type=jnp.float32,
    )
    masked = correlation * live_slots.astype(jnp.float32)[:, None, None, None]
    return masked.astype(jnp.bfloat16)[None]


def solution(mesh):
    pairs_count, win_count = mesh.devices.shape
    side = math.isqrt(win_count)
    grid = Mesh(mesh.devices.reshape(pairs_count, side, side), ("pairs", "z", "y"))
    in_specs = (P("pairs", ("z", "y"), None, None), P(), P())
    out_specs = P("pairs", None, ("z", "y"), None, None)
    return jax.shard_map(shards, mesh=grid, in_specs=in_specs, out_specs=out_specs, check_vma=False)
```

```python
import math

import jax
import jax.numpy as jnp
import ml_dtypes
import numpy as np
from jax import lax
from jax.sharding import Mesh
from jax.sharding import PartitionSpec as P

NSAMP = 4096
FREQS = 32
LOW_BIN = 16
LAGS = 128


WATER = 0.1


def band_table():
    sample_idx = np.arange(NSAMP, dtype=np.int64)
    bin_idx = np.arange(FREQS, dtype=np.int64) + LOW_BIN
    phase = (sample_idx[:, None] * bin_idx[None, :] % NSAMP).astype(np.float64) * (
        2.0 * math.pi / NSAMP
    )
    scaled = np.concatenate([np.cos(phase), -np.sin(phase)], axis=1) * (1.0 / math.sqrt(NSAMP))
    return jnp.asarray(scaled.astype(ml_dtypes.bfloat16))


def lag_table(segments):
    bin_idx = jnp.arange(FREQS, dtype=jnp.int32) + LOW_BIN
    lag_idx = (jnp.arange(LAGS, dtype=jnp.int32) - LAGS // 2) * (NSAMP // LAGS)
    phase = (bin_idx[:, None] * lag_idx[None, :] % NSAMP).astype(jnp.float32) * (
        2.0 * math.pi / NSAMP
    )
    return jnp.concatenate([jnp.cos(phase), -jnp.sin(phase)], axis=0) * (
        1.0 / math.sqrt(segments * FREQS)
    )


def whiten(spectra):
    real_part = spectra[..., :FREQS]
    imag_part = spectra[..., FREQS:]
    power_bins = real_part * real_part + imag_part * imag_part
    widths = [(0, 0)] * (power_bins.ndim - 1) + [(2, 2)]
    padded = jnp.pad(power_bins, widths)
    smooth = (
        padded[..., 0:FREQS]
        + padded[..., 1 : FREQS + 1]
        + padded[..., 2 : FREQS + 2]
        + padded[..., 3 : FREQS + 3]
        + padded[..., 4 : FREQS + 4]
    ) * 0.2
    water_level = smooth + WATER * jnp.mean(power_bins, axis=-1, keepdims=True) + 1e-06
    factor = lax.rsqrt(water_level)
    return jnp.concatenate([real_part * factor, imag_part * factor], axis=-1).astype(jnp.bfloat16)


def shards(records, pair_list, pair_count):
    seg_dev = records.shape[1]
    block_width = records.shape[2]
    slot_count = pair_list.shape[1]
    pairs_count = lax.axis_size("pairs")
    side = lax.axis_size("y")
    rows = block_width // (side * side)
    chips = pairs_count // 2
    width = 2 * FREQS
    spec_rows = seg_dev * width
    half_rows = spec_rows // 2
    spectra = whiten(jnp.dot(records[0], band_table(), preferred_element_type=jnp.float32))
    own = jnp.transpose(spectra, (0, 2, 1)).reshape(spec_rows, block_width)
    owner_index = lax.axis_index("pairs")
    core = owner_index % 2
    chip = owner_index // 2
    first_core = core == 0
    z_index = lax.axis_index("z")
    y_index = lax.axis_index("y")
    gather_pos = jnp.where(first_core, y_index, z_index)
    reduce_pos = jnp.where(first_core, z_index, y_index)

    swap = [(p, p ^ 1) for p in range(pairs_count)]

    def chip_shift(d):
        return [(p, 2 * ((p // 2 + d) % chips) + p % 2) for p in range(pairs_count)]

    partner = lax.ppermute(own, "pairs", swap)
    from_below = lax.ppermute(own, "pairs", chip_shift(1))
    from_above = lax.ppermute(own, "pairs", chip_shift(-1))
    from_far = lax.ppermute(own, "pairs", chip_shift(2))
    mine = jnp.stack([own, from_above, from_far, from_below])
    theirs = lax.ppermute(mine[1:], "pairs", swap)
    theirs = jnp.concatenate([partner[None], theirs])
    table = jnp.concatenate([mine, theirs])
    own_pairs = lax.dynamic_index_in_dim(pair_list, owner_index, 0, keepdims=False)
    live_slots = jnp.arange(slot_count, dtype=jnp.int32) < pair_count[owner_index]
    position = (own_pairs // 2 - chip) % chips + chips * (own_pairs % 2 != core)
    chosen = jnp.take(table, position.T.reshape(-1), axis=0, mode="clip")
    left = chosen[:slot_count]
    right = chosen[slot_count:]
    left_t = jnp.transpose(left, (0, 2, 1)).reshape((slot_count, side, side, rows, spec_rows))
    left_t = jnp.where(first_core, jnp.swapaxes(left_t, 1, 2), left_t)
    packed_rows = spec_rows * side * rows // block_width
    packs = jnp.transpose(left_t, (1, 0, 2, 3, 4)).reshape(
        (side, slot_count, packed_rows, block_width)
    )

    def rows_for(pos):
        return lax.dynamic_index_in_dim(packs, pos, 0, keepdims=False)

    def gather_perm(d):
        perm = []
        for p in range(pairs_count):
            for z in range(side):
                for y in range(side):
                    src = (p * side + z) * side + y
                    if p % 2 == 0:
                        dst = (p * side + z) * side + (y + d) % side
                    else:
                        dst = (p * side + (z + d) % side) * side + y
                    perm.append((src, dst))
        return perm

    def reduce_perm(e):
        perm = []
        for p in range(pairs_count):
            for z in range(side):
                for y in range(side):
                    src = (p * side + z) * side + y
                    if p % 2 == 0:
                        dst = (p * side + (z + e) % side) * side + y
                    else:
                        dst = (p * side + z) * side + (y + e) % side
                    perm.append((src, dst))
        return perm

    axes = ("pairs", "z", "y")
    pieces = [jnp.concatenate([right, rows_for(gather_pos)], axis=1)]
    for d in sorted(range(1, side), key=lambda step: -min(step, side - step)):
        message = jnp.concatenate([right, rows_for((gather_pos + d) % side)], axis=1)
        pieces.append(lax.ppermute(message, axes, gather_perm(d)))
    gathered = jnp.stack(pieces)
    right_all = gathered[:, :, :spec_rows].reshape(
        (side, slot_count, seg_dev, 2, FREQS, block_width)
    )
    left_all = gathered[:, :, spec_rows:].reshape((side, slot_count, side * rows, seg_dev, 2, FREQS))
    left_all = jnp.transpose(left_all, (0, 1, 3, 4, 5, 2))
    right_swapped = jnp.stack([right_all[:, :, :, 1], -right_all[:, :, :, 0]], axis=3)
    rhs = jnp.concatenate([right_all, right_swapped], axis=-1)
    partial_value = jnp.einsum(
        "akscfm,akscfn->kfmn", left_all, rhs, preferred_element_type=jnp.float32
    )
    partial_value = partial_value.reshape((slot_count, FREQS, side, rows, 2, block_width))
    partial_value = jnp.transpose(partial_value, (2, 0, 4, 1, 3, 5)).astype(jnp.bfloat16)
    chunk_rows = slot_count * 2 * FREQS * rows
    partial_value = partial_value.reshape((side, chunk_rows, block_width))
    stacked = lax.dynamic_index_in_dim(partial_value, reduce_pos, 0, keepdims=False).astype(
        jnp.float32
    )
    for e in sorted(range(1, side), key=lambda step: -min(step, side - step)):
        chunk = lax.dynamic_index_in_dim(partial_value, (reduce_pos + e) % side, 0, keepdims=False)
        stacked = stacked + lax.ppermute(chunk, axes, reduce_perm(e)).astype(jnp.float32)
    stacked = stacked.reshape((slot_count, 2, FREQS, rows, block_width))
    lag_weights = lag_table(seg_dev * side * side).reshape(2, FREQS, LAGS)
    correlation = jnp.einsum(
        "kpfrj,pft->krjt",
        stacked,
        lag_weights,
        precision=lax.Precision.DEFAULT,
        preferred_element_type=jnp.float32,
    )
    masked = correlation * live_slots.astype(jnp.float32)[:, None, None, None]
    return masked.astype(jnp.bfloat16)[None]


def solution(mesh):
    pairs_count, win_count = mesh.devices.shape
    side = math.isqrt(win_count)
    grid = Mesh(mesh.devices.reshape(pairs_count, side, side), ("pairs", "z", "y"))
    in_specs = (P("pairs", ("z", "y"), None, None), P(), P())
    out_specs = P("pairs", None, ("z", "y"), None, None)
    return jax.shard_map(shards, mesh=grid, in_specs=in_specs, out_specs=out_specs, check_vma=False)
```

```python
import math

import jax
import jax.numpy as jnp
import ml_dtypes
import numpy as np
from jax import lax
from jax.sharding import Mesh
from jax.sharding import PartitionSpec as P

NSAMP = 4096
FREQS = 32
LOW_BIN = 16
LAGS = 128


WATER = 0.1


def band_table():
    sample_idx = np.arange(NSAMP, dtype=np.int64)
    bin_idx = np.arange(FREQS, dtype=np.int64) + LOW_BIN
    phase = (sample_idx[:, None] * bin_idx[None, :] % NSAMP).astype(np.float64) * (
        2.0 * math.pi / NSAMP
    )
    scaled = np.concatenate([np.cos(phase), -np.sin(phase)], axis=1) * (1.0 / math.sqrt(NSAMP))
    return jnp.asarray(scaled.astype(ml_dtypes.bfloat16))


def lag_table(segments):
    bin_idx = jnp.arange(FREQS, dtype=jnp.int32) + LOW_BIN
    lag_idx = (jnp.arange(LAGS, dtype=jnp.int32) - LAGS // 2) * (NSAMP // LAGS)
    phase = (bin_idx[:, None] * lag_idx[None, :] % NSAMP).astype(jnp.float32) * (
        2.0 * math.pi / NSAMP
    )
    return jnp.concatenate([jnp.cos(phase), -jnp.sin(phase)], axis=0) * (
        1.0 / math.sqrt(segments * FREQS)
    )


def whiten(spectra):
    real_part = spectra[..., :FREQS]
    imag_part = spectra[..., FREQS:]
    power_bins = real_part * real_part + imag_part * imag_part
    widths = [(0, 0)] * (power_bins.ndim - 1) + [(2, 2)]
    padded = jnp.pad(power_bins, widths)
    smooth = (
        padded[..., 0:FREQS]
        + padded[..., 1 : FREQS + 1]
        + padded[..., 2 : FREQS + 2]
        + padded[..., 3 : FREQS + 3]
        + padded[..., 4 : FREQS + 4]
    ) * 0.2
    water_level = smooth + WATER * jnp.mean(power_bins, axis=-1, keepdims=True) + 1e-06
    factor = lax.rsqrt(water_level)
    return jnp.concatenate([real_part * factor, imag_part * factor], axis=-1).astype(jnp.bfloat16)


def shards(records, pair_list, pair_count):
    seg_dev = records.shape[1]
    block_width = records.shape[2]
    slot_count = pair_list.shape[1]
    pairs_count = lax.axis_size("pairs")
    side = lax.axis_size("y")
    rows = block_width // (side * side)
    chips = pairs_count // 2
    width = 2 * FREQS
    spec_rows = seg_dev * width
    half_rows = spec_rows // 2
    spectra = whiten(jnp.dot(records[0], band_table(), preferred_element_type=jnp.float32))
    own = jnp.transpose(spectra, (0, 2, 1)).reshape(spec_rows, block_width)
    owner_index = lax.axis_index("pairs")
    core = owner_index % 2
    chip = owner_index // 2
    first_core = core == 0
    z_index = lax.axis_index("z")
    y_index = lax.axis_index("y")
    gather_pos = jnp.where(first_core, y_index, z_index)
    reduce_pos = jnp.where(first_core, z_index, y_index)

    swap = [(p, p ^ 1) for p in range(pairs_count)]

    def chip_shift(d):
        return [(p, 2 * ((p // 2 + d) % chips) + p % 2) for p in range(pairs_count)]

    partner = lax.ppermute(own, "pairs", swap)
    from_below = lax.ppermute(own, "pairs", chip_shift(1))
    from_above = lax.ppermute(own, "pairs", chip_shift(-1))
    from_far = lax.ppermute(own, "pairs", chip_shift(2))
    mine = jnp.stack([own, from_above, from_far, from_below])
    theirs_near = lax.ppermute(jnp.stack([from_above, from_below]), "pairs", swap)
    theirs_far = lax.ppermute(from_far, "pairs", swap)
    theirs = jnp.stack([partner, theirs_near[0], theirs_far, theirs_near[1]])
    table = jnp.where(
        first_core, jnp.stack([mine, theirs], axis=1), jnp.stack([theirs, mine], axis=1)
    ).reshape((pairs_count,) + own.shape)
    own_pairs = lax.dynamic_index_in_dim(pair_list, owner_index, 0, keepdims=False)
    live_slots = jnp.arange(slot_count, dtype=jnp.int32) < pair_count[owner_index]
    position = ((own_pairs // 2 - chip) % chips) * 2 + own_pairs % 2
    chosen = jnp.take(table, position.T.reshape(-1), axis=0)
    left = chosen[:slot_count]
    right = chosen[slot_count:]
    left_t = jnp.transpose(left, (0, 2, 1)).reshape((slot_count, side, side, rows, spec_rows))
    left_t = jnp.where(first_core, jnp.swapaxes(left_t, 1, 2), left_t)
    packed_rows = spec_rows * side * rows // block_width
    packs = jnp.transpose(left_t, (1, 0, 2, 3, 4)).reshape(
        (side, slot_count, packed_rows, block_width)
    )

    def rows_for(pos):
        return lax.dynamic_index_in_dim(packs, pos, 0, keepdims=False)

    def gather_perm(d):
        perm = []
        for p in range(pairs_count):
            for z in range(side):
                for y in range(side):
                    src = (p * side + z) * side + y
                    if p % 2 == 0:
                        dst = (p * side + z) * side + (y + d) % side
                    else:
                        dst = (p * side + (z + d) % side) * side + y
                    perm.append((src, dst))
        return perm

    def reduce_perm(e):
        perm = []
        for p in range(pairs_count):
            for z in range(side):
                for y in range(side):
                    src = (p * side + z) * side + y
                    if p % 2 == 0:
                        dst = (p * side + (z + e) % side) * side + y
                    else:
                        dst = (p * side + z) * side + (y + e) % side
                    perm.append((src, dst))
        return perm

    axes = ("pairs", "z", "y")
    pieces = [jnp.concatenate([right, rows_for(gather_pos)], axis=1)]
    for d in sorted(range(1, side), key=lambda step: -min(step, side - step)):
        message = jnp.concatenate([right, rows_for((gather_pos + d) % side)], axis=1)
        pieces.append(lax.ppermute(message, axes, gather_perm(d)))
    gathered = jnp.stack(pieces)
    right_all = gathered[:, :, :spec_rows].reshape(
        (side, slot_count, seg_dev, 2, FREQS, block_width)
    )
    left_all = gathered[:, :, spec_rows:].reshape((side, slot_count, side * rows, seg_dev, 2, FREQS))
    left_all = jnp.transpose(left_all, (0, 1, 3, 4, 5, 2))
    right_swapped = jnp.stack([right_all[:, :, :, 1], -right_all[:, :, :, 0]], axis=3)
    rhs = jnp.concatenate([right_all, right_swapped], axis=-1)
    partial_value = jnp.einsum(
        "akscfm,akscfn->kfmn", left_all, rhs, preferred_element_type=jnp.float32
    )
    partial_value = partial_value.reshape((slot_count, FREQS, side, rows, 2, block_width))
    partial_value = jnp.transpose(partial_value, (2, 0, 4, 1, 3, 5)).astype(jnp.bfloat16)
    chunk_rows = slot_count * 2 * FREQS * rows
    partial_value = partial_value.reshape((side, chunk_rows, block_width))
    stacked = lax.dynamic_index_in_dim(partial_value, reduce_pos, 0, keepdims=False).astype(
        jnp.float32
    )
    for e in sorted(range(1, side), key=lambda step: -min(step, side - step)):
        chunk = lax.dynamic_index_in_dim(partial_value, (reduce_pos + e) % side, 0, keepdims=False)
        stacked = stacked + lax.ppermute(chunk, axes, reduce_perm(e)).astype(jnp.float32)
    stacked = stacked.reshape((slot_count, 2, FREQS, rows, block_width))
    lag_weights = lag_table(seg_dev * side * side).reshape(2, FREQS, LAGS)
    correlation = jnp.einsum(
        "kpfrj,pft->krjt",
        stacked,
        lag_weights,
        precision=lax.Precision.DEFAULT,
        preferred_element_type=jnp.float32,
    )
    masked = correlation * live_slots.astype(jnp.float32)[:, None, None, None]
    return masked.astype(jnp.bfloat16)[None]


def solution(mesh):
    pairs_count, win_count = mesh.devices.shape
    side = math.isqrt(win_count)
    grid = Mesh(mesh.devices.reshape(pairs_count, side, side), ("pairs", "z", "y"))
    in_specs = (P("pairs", ("z", "y"), None, None), P(), P())
    out_specs = P("pairs", None, ("z", "y"), None, None)
    return jax.shard_map(shards, mesh=grid, in_specs=in_specs, out_specs=out_specs, check_vma=False)
```

```python
import math

import jax
import jax.numpy as jnp
import ml_dtypes
import numpy as np
from jax import lax
from jax.sharding import Mesh
from jax.sharding import PartitionSpec as P

NSAMP = 4096
FREQS = 32
LOW_BIN = 16
LAGS = 128


WATER = 0.1


def band_table():
    sample_idx = np.arange(NSAMP, dtype=np.int64)
    bin_idx = np.arange(FREQS, dtype=np.int64) + LOW_BIN
    phase = (sample_idx[:, None] * bin_idx[None, :] % NSAMP).astype(np.float64) * (
        2.0 * math.pi / NSAMP
    )
    scaled = np.concatenate([np.cos(phase), -np.sin(phase)], axis=1) * (1.0 / math.sqrt(NSAMP))
    return jnp.asarray(scaled.astype(ml_dtypes.bfloat16))


def lag_table(segments):
    bin_idx = jnp.arange(FREQS, dtype=jnp.int32) + LOW_BIN
    lag_idx = (jnp.arange(LAGS, dtype=jnp.int32) - LAGS // 2) * (NSAMP // LAGS)
    phase = (bin_idx[:, None] * lag_idx[None, :] % NSAMP).astype(jnp.float32) * (
        2.0 * math.pi / NSAMP
    )
    return jnp.concatenate([jnp.cos(phase), -jnp.sin(phase)], axis=0) * (
        1.0 / math.sqrt(segments * FREQS)
    )


def whiten(spectra):
    real_part = spectra[..., :FREQS]
    imag_part = spectra[..., FREQS:]
    power_bins = real_part * real_part + imag_part * imag_part
    widths = [(0, 0)] * (power_bins.ndim - 1) + [(2, 2)]
    padded = jnp.pad(power_bins, widths)
    smooth = (
        padded[..., 0:FREQS]
        + padded[..., 1 : FREQS + 1]
        + padded[..., 2 : FREQS + 2]
        + padded[..., 3 : FREQS + 3]
        + padded[..., 4 : FREQS + 4]
    ) * 0.2
    water_level = smooth + WATER * jnp.mean(power_bins, axis=-1, keepdims=True) + 1e-06
    factor = lax.rsqrt(water_level)
    return jnp.concatenate([real_part * factor, imag_part * factor], axis=-1).astype(jnp.bfloat16)


def shards(records, pair_list, pair_count):
    seg_dev = records.shape[1]
    block_width = records.shape[2]
    slot_count = pair_list.shape[1]
    pairs_count = lax.axis_size("pairs")
    side = lax.axis_size("y")
    rows = block_width // (side * side)
    chips = pairs_count // 2
    width = 2 * FREQS
    spec_rows = seg_dev * width
    half_rows = spec_rows // 2
    spectra = whiten(jnp.dot(records[0], band_table(), preferred_element_type=jnp.float32))
    own = jnp.transpose(spectra, (0, 2, 1)).reshape(spec_rows, block_width)
    owner_index = lax.axis_index("pairs")
    core = owner_index % 2
    chip = owner_index // 2
    first_core = core == 0
    z_index = lax.axis_index("z")
    y_index = lax.axis_index("y")
    gather_pos = jnp.where(first_core, y_index, z_index)
    reduce_pos = jnp.where(first_core, z_index, y_index)

    swap = [(p, p ^ 1) for p in range(pairs_count)]

    def chip_shift(d):
        return [(p, 2 * ((p // 2 + d) % chips) + p % 2) for p in range(pairs_count)]

    from_far = lax.ppermute(own, "pairs", chip_shift(2))
    partner = lax.ppermute(own, "pairs", swap)
    own_near = own + jnp.zeros((), own.dtype) * partner[:1, :1]
    from_below = lax.ppermute(own_near, "pairs", chip_shift(1))
    from_above = lax.ppermute(own_near, "pairs", chip_shift(-1))
    mine = jnp.stack([own, from_above, from_far, from_below])
    theirs_near = lax.ppermute(jnp.stack([from_above, from_below]), "pairs", swap)
    theirs_far = lax.ppermute(from_far, "pairs", swap)
    theirs = jnp.stack([partner, theirs_near[0], theirs_far, theirs_near[1]])
    table = jnp.where(
        first_core, jnp.stack([mine, theirs], axis=1), jnp.stack([theirs, mine], axis=1)
    ).reshape((pairs_count,) + own.shape)
    own_pairs = lax.dynamic_index_in_dim(pair_list, owner_index, 0, keepdims=False)
    live_slots = jnp.arange(slot_count, dtype=jnp.int32) < pair_count[owner_index]
    position = ((own_pairs // 2 - chip) % chips) * 2 + own_pairs % 2
    chosen = jnp.take(table, position.T.reshape(-1), axis=0)
    left = chosen[:slot_count]
    right = chosen[slot_count:]
    left_t = jnp.transpose(left, (0, 2, 1)).reshape((slot_count, side, side, rows, spec_rows))
    left_t = jnp.where(first_core, jnp.swapaxes(left_t, 1, 2), left_t)
    packed_rows = spec_rows * side * rows // block_width
    packs = jnp.transpose(left_t, (1, 0, 2, 3, 4)).reshape(
        (side, slot_count, packed_rows, block_width)
    )

    def rows_for(pos):
        return lax.dynamic_index_in_dim(packs, pos, 0, keepdims=False)

    def gather_perm(d):
        perm = []
        for p in range(pairs_count):
            for z in range(side):
                for y in range(side):
                    src = (p * side + z) * side + y
                    if p % 2 == 0:
                        dst = (p * side + z) * side + (y + d) % side
                    else:
                        dst = (p * side + (z + d) % side) * side + y
                    perm.append((src, dst))
        return perm

    def reduce_perm(e):
        perm = []
        for p in range(pairs_count):
            for z in range(side):
                for y in range(side):
                    src = (p * side + z) * side + y
                    if p % 2 == 0:
                        dst = (p * side + (z + e) % side) * side + y
                    else:
                        dst = (p * side + z) * side + (y + e) % side
                    perm.append((src, dst))
        return perm

    axes = ("pairs", "z", "y")
    pieces = [jnp.concatenate([right, rows_for(gather_pos)], axis=1)]
    for d in sorted(range(1, side), key=lambda step: -min(step, side - step)):
        message = jnp.concatenate([right, rows_for((gather_pos + d) % side)], axis=1)
        pieces.append(lax.ppermute(message, axes, gather_perm(d)))
    gathered = jnp.stack(pieces)
    right_all = gathered[:, :, :spec_rows].reshape(
        (side, slot_count, seg_dev, 2, FREQS, block_width)
    )
    left_all = gathered[:, :, spec_rows:].reshape((side, slot_count, side * rows, seg_dev, 2, FREQS))
    left_all = jnp.transpose(left_all, (0, 1, 3, 4, 5, 2))
    right_swapped = jnp.stack([right_all[:, :, :, 1], -right_all[:, :, :, 0]], axis=3)
    rhs = jnp.concatenate([right_all, right_swapped], axis=-1)
    partial_value = jnp.einsum(
        "akscfm,akscfn->kfmn", left_all, rhs, preferred_element_type=jnp.float32
    )
    partial_value = partial_value.reshape((slot_count, FREQS, side, rows, 2, block_width))
    partial_value = jnp.transpose(partial_value, (2, 0, 4, 1, 3, 5)).astype(jnp.bfloat16)
    chunk_rows = slot_count * 2 * FREQS * rows
    partial_value = partial_value.reshape((side, chunk_rows, block_width))
    stacked = lax.dynamic_index_in_dim(partial_value, reduce_pos, 0, keepdims=False).astype(
        jnp.float32
    )
    for e in sorted(range(1, side), key=lambda step: -min(step, side - step)):
        chunk = lax.dynamic_index_in_dim(partial_value, (reduce_pos + e) % side, 0, keepdims=False)
        stacked = stacked + lax.ppermute(chunk, axes, reduce_perm(e)).astype(jnp.float32)
    stacked = stacked.reshape((slot_count, 2, FREQS, rows, block_width))
    lag_weights = lag_table(seg_dev * side * side).reshape(2, FREQS, LAGS)
    correlation = jnp.einsum(
        "kpfrj,pft->krjt",
        stacked,
        lag_weights,
        precision=lax.Precision.DEFAULT,
        preferred_element_type=jnp.float32,
    )
    masked = correlation * live_slots.astype(jnp.float32)[:, None, None, None]
    return masked.astype(jnp.bfloat16)[None]


def solution(mesh):
    pairs_count, win_count = mesh.devices.shape
    side = math.isqrt(win_count)
    grid = Mesh(mesh.devices.reshape(pairs_count, side, side), ("pairs", "z", "y"))
    in_specs = (P("pairs", ("z", "y"), None, None), P(), P())
    out_specs = P("pairs", None, ("z", "y"), None, None)
    return jax.shard_map(shards, mesh=grid, in_specs=in_specs, out_specs=out_specs, check_vma=False)
```

```python
import math

import jax
import jax.numpy as jnp
import ml_dtypes
import numpy as np
from jax import lax
from jax.sharding import Mesh
from jax.sharding import PartitionSpec as P

NSAMP = 4096
FREQS = 32
LOW_BIN = 16
LAGS = 128


WATER = 0.1


def band_table():
    sample_idx = np.arange(NSAMP, dtype=np.int64)
    bin_idx = np.arange(FREQS, dtype=np.int64) + LOW_BIN
    phase = (sample_idx[:, None] * bin_idx[None, :] % NSAMP).astype(np.float64) * (
        2.0 * math.pi / NSAMP
    )
    scaled = np.concatenate([np.cos(phase), -np.sin(phase)], axis=1) * (1.0 / math.sqrt(NSAMP))
    return jnp.asarray(scaled.astype(ml_dtypes.bfloat16))


def lag_table(segments):
    bin_idx = jnp.arange(FREQS, dtype=jnp.int32) + LOW_BIN
    lag_idx = (jnp.arange(LAGS, dtype=jnp.int32) - LAGS // 2) * (NSAMP // LAGS)
    phase = (bin_idx[:, None] * lag_idx[None, :] % NSAMP).astype(jnp.float32) * (
        2.0 * math.pi / NSAMP
    )
    return jnp.concatenate([jnp.cos(phase), -jnp.sin(phase)], axis=0) * (
        1.0 / math.sqrt(segments * FREQS)
    )


def whiten(spectra):
    real_part = spectra[..., :FREQS]
    imag_part = spectra[..., FREQS:]
    power_bins = real_part * real_part + imag_part * imag_part
    widths = [(0, 0)] * (power_bins.ndim - 1) + [(2, 2)]
    padded = jnp.pad(power_bins, widths)
    smooth = (
        padded[..., 0:FREQS]
        + padded[..., 1 : FREQS + 1]
        + padded[..., 2 : FREQS + 2]
        + padded[..., 3 : FREQS + 3]
        + padded[..., 4 : FREQS + 4]
    ) * 0.2
    water_level = smooth + WATER * jnp.mean(power_bins, axis=-1, keepdims=True) + 1e-06
    factor = lax.rsqrt(water_level)
    return jnp.concatenate([real_part * factor, imag_part * factor], axis=-1).astype(jnp.bfloat16)


def shards(records, pair_list, pair_count):
    seg_dev = records.shape[1]
    block_width = records.shape[2]
    slot_count = pair_list.shape[1]
    pairs_count = lax.axis_size("pairs")
    side = lax.axis_size("y")
    rows = block_width // (side * side)
    chips = pairs_count // 2
    width = 2 * FREQS
    spec_rows = seg_dev * width
    half_rows = spec_rows // 2
    spectra = whiten(jnp.dot(records[0], band_table(), preferred_element_type=jnp.float32))
    own = jnp.transpose(spectra, (0, 2, 1)).reshape(spec_rows, block_width)
    owner_index = lax.axis_index("pairs")
    core = owner_index % 2
    chip = owner_index // 2
    first_core = core == 0
    z_index = lax.axis_index("z")
    y_index = lax.axis_index("y")
    gather_pos = jnp.where(first_core, y_index, z_index)
    reduce_pos = jnp.where(first_core, z_index, y_index)

    swap = [(p, p ^ 1) for p in range(pairs_count)]

    def chip_shift(d):
        return [(p, 2 * ((p // 2 + d) % chips) + p % 2) for p in range(pairs_count)]

    partner = lax.ppermute(own, "pairs", swap)
    from_below = lax.ppermute(own, "pairs", chip_shift(1))
    from_above = lax.ppermute(own, "pairs", chip_shift(-1))
    from_far = lax.ppermute(own, "pairs", chip_shift(2))
    mine = jnp.stack([own, from_above, from_far, from_below])
    theirs_near = lax.ppermute(jnp.stack([from_above, from_below]), "pairs", swap)
    theirs_far = lax.ppermute(from_far, "pairs", swap)
    theirs = jnp.stack([partner, theirs_near[0], theirs_far, theirs_near[1]])
    table = jnp.where(
        first_core, jnp.stack([mine, theirs], axis=1), jnp.stack([theirs, mine], axis=1)
    ).reshape((pairs_count,) + own.shape)
    own_pairs = lax.dynamic_index_in_dim(pair_list, owner_index, 0, keepdims=False)
    live_slots = jnp.arange(slot_count, dtype=jnp.int32) < pair_count[owner_index]
    position = ((own_pairs // 2 - chip) % chips) * 2 + own_pairs % 2
    chosen = jnp.take(table, position.T.reshape(-1), axis=0, mode="clip")
    left = chosen[:slot_count]
    right = chosen[slot_count:]
    left_t = jnp.transpose(left, (0, 2, 1)).reshape((slot_count, side, side, rows, spec_rows))
    left_t = jnp.where(first_core, jnp.swapaxes(left_t, 1, 2), left_t)
    packed_rows = spec_rows * side * rows // block_width
    packs = jnp.transpose(left_t, (1, 0, 2, 3, 4)).reshape(
        (side, slot_count, packed_rows, block_width)
    )

    def rows_for(pos):
        return lax.dynamic_index_in_dim(packs, pos, 0, keepdims=False)

    def gather_perm(d):
        perm = []
        for p in range(pairs_count):
            for z in range(side):
                for y in range(side):
                    src = (p * side + z) * side + y
                    if p % 2 == 0:
                        dst = (p * side + z) * side + (y + d) % side
                    else:
                        dst = (p * side + (z + d) % side) * side + y
                    perm.append((src, dst))
        return perm

    def reduce_perm(e):
        perm = []
        for p in range(pairs_count):
            for z in range(side):
                for y in range(side):
                    src = (p * side + z) * side + y
                    if p % 2 == 0:
                        dst = (p * side + (z + e) % side) * side + y
                    else:
                        dst = (p * side + z) * side + (y + e) % side
                    perm.append((src, dst))
        return perm

    axes = ("pairs", "z", "y")
    pieces = [jnp.concatenate([right, rows_for(gather_pos)], axis=1)]
    for d in sorted(range(1, side), key=lambda step: -min(step, side - step)):
        message = jnp.concatenate([right, rows_for((gather_pos + d) % side)], axis=1)
        pieces.append(lax.ppermute(message, axes, gather_perm(d)))
    gathered = jnp.stack(pieces)
    right_all = gathered[:, :, :spec_rows].reshape(
        (side, slot_count, seg_dev, 2, FREQS, block_width)
    )
    left_all = gathered[:, :, spec_rows:].reshape((side, slot_count, side * rows, seg_dev, 2, FREQS))
    left_all = jnp.transpose(left_all, (0, 1, 3, 4, 5, 2))
    right_swapped = jnp.stack([right_all[:, :, :, 1], -right_all[:, :, :, 0]], axis=3)
    rhs = jnp.concatenate([right_all, right_swapped], axis=-1)
    partial_value = jnp.einsum(
        "akscfm,akscfn->kfmn", left_all, rhs, preferred_element_type=jnp.float32
    )
    partial_value = partial_value.reshape((slot_count, FREQS, side, rows, 2, block_width))
    partial_value = jnp.transpose(partial_value, (2, 0, 4, 1, 3, 5)).astype(jnp.bfloat16)
    chunk_rows = slot_count * 2 * FREQS * rows
    partial_value = partial_value.reshape((side, chunk_rows, block_width))
    stacked = lax.dynamic_index_in_dim(partial_value, reduce_pos, 0, keepdims=False).astype(
        jnp.float32
    )
    for e in sorted(range(1, side), key=lambda step: -min(step, side - step)):
        chunk = lax.dynamic_index_in_dim(partial_value, (reduce_pos + e) % side, 0, keepdims=False)
        stacked = stacked + lax.ppermute(chunk, axes, reduce_perm(e)).astype(jnp.float32)
    stacked = stacked.reshape((slot_count, 2, FREQS, rows, block_width))
    lag_weights = lag_table(seg_dev * side * side).reshape(2, FREQS, LAGS)
    correlation = jnp.einsum(
        "kpfrj,pft->krjt",
        stacked,
        lag_weights,
        precision=lax.Precision.DEFAULT,
        preferred_element_type=jnp.float32,
    )
    masked = correlation * live_slots.astype(jnp.float32)[:, None, None, None]
    return masked.astype(jnp.bfloat16)[None]


def solution(mesh):
    pairs_count, win_count = mesh.devices.shape
    side = math.isqrt(win_count)
    grid = Mesh(mesh.devices.reshape(pairs_count, side, side), ("pairs", "z", "y"))
    in_specs = (P("pairs", ("z", "y"), None, None), P(), P())
    out_specs = P("pairs", None, ("z", "y"), None, None)
    return jax.shard_map(shards, mesh=grid, in_specs=in_specs, out_specs=out_specs, check_vma=False)
```

```python
import math

import jax
import jax.numpy as jnp
import ml_dtypes
import numpy as np
from jax import lax
from jax.sharding import Mesh
from jax.sharding import PartitionSpec as P

NSAMP = 4096
FREQS = 32
LOW_BIN = 16
LAGS = 128


WATER = 0.1


def band_table():
    sample_idx = np.arange(NSAMP, dtype=np.int64)
    bin_idx = np.arange(FREQS, dtype=np.int64) + LOW_BIN
    phase = (sample_idx[:, None] * bin_idx[None, :] % NSAMP).astype(np.float64) * (
        2.0 * math.pi / NSAMP
    )
    scaled = np.concatenate([np.cos(phase), -np.sin(phase)], axis=1) * (1.0 / math.sqrt(NSAMP))
    return jnp.asarray(scaled.astype(ml_dtypes.bfloat16))


def lag_table(segments):
    bin_idx = jnp.arange(FREQS, dtype=jnp.int32) + LOW_BIN
    lag_idx = (jnp.arange(LAGS, dtype=jnp.int32) - LAGS // 2) * (NSAMP // LAGS)
    phase = (bin_idx[:, None] * lag_idx[None, :] % NSAMP).astype(jnp.float32) * (
        2.0 * math.pi / NSAMP
    )
    return jnp.concatenate([jnp.cos(phase), -jnp.sin(phase)], axis=0) * (
        1.0 / math.sqrt(segments * FREQS)
    )


def whiten(spectra):
    real_part = spectra[..., :FREQS]
    imag_part = spectra[..., FREQS:]
    power_bins = real_part * real_part + imag_part * imag_part
    widths = [(0, 0)] * (power_bins.ndim - 1) + [(2, 2)]
    padded = jnp.pad(power_bins, widths)
    smooth = (
        padded[..., 0:FREQS]
        + padded[..., 1 : FREQS + 1]
        + padded[..., 2 : FREQS + 2]
        + padded[..., 3 : FREQS + 3]
        + padded[..., 4 : FREQS + 4]
    ) * 0.2
    water_level = smooth + WATER * jnp.mean(power_bins, axis=-1, keepdims=True) + 1e-06
    factor = lax.rsqrt(water_level)
    return jnp.concatenate([real_part * factor, imag_part * factor], axis=-1).astype(jnp.bfloat16)


def shards(records, pair_list, pair_count):
    seg_dev = records.shape[1]
    block_width = records.shape[2]
    slot_count = pair_list.shape[1]
    pairs_count = lax.axis_size("pairs")
    side = lax.axis_size("y")
    rows = block_width // (side * side)
    chips = pairs_count // 2
    width = 2 * FREQS
    spec_rows = seg_dev * width
    half_rows = spec_rows // 2
    spectra = whiten(jnp.dot(records[0], band_table(), preferred_element_type=jnp.float32))
    own = jnp.transpose(spectra, (0, 2, 1)).reshape(spec_rows, block_width)
    owner_index = lax.axis_index("pairs")
    core = owner_index % 2
    chip = owner_index // 2
    first_core = core == 0
    z_index = lax.axis_index("z")
    y_index = lax.axis_index("y")
    gather_pos = jnp.where(first_core, y_index, z_index)
    reduce_pos = jnp.where(first_core, z_index, y_index)

    swap = [(p, p ^ 1) for p in range(pairs_count)]

    def chip_shift(d):
        return [(p, 2 * ((p // 2 + d) % chips) + p % 2) for p in range(pairs_count)]

    partner = lax.ppermute(own, "pairs", swap)
    from_below = lax.ppermute(own, "pairs", chip_shift(1))
    from_above = lax.ppermute(own, "pairs", chip_shift(-1))
    from_far = lax.ppermute(own, "pairs", chip_shift(2))
    mine = jnp.stack([own, from_above, from_far, from_below])
    theirs_above = lax.ppermute(from_above, "pairs", swap)
    theirs_below = lax.ppermute(from_below, "pairs", swap)
    theirs_far = lax.ppermute(from_far, "pairs", swap)
    theirs = jnp.stack([partner, theirs_above, theirs_far, theirs_below])
    table = jnp.where(
        first_core, jnp.stack([mine, theirs], axis=1), jnp.stack([theirs, mine], axis=1)
    ).reshape((pairs_count,) + own.shape)
    own_pairs = lax.dynamic_index_in_dim(pair_list, owner_index, 0, keepdims=False)
    live_slots = jnp.arange(slot_count, dtype=jnp.int32) < pair_count[owner_index]
    position = ((own_pairs // 2 - chip) % chips) * 2 + own_pairs % 2
    chosen = jnp.take(table, position.T.reshape(-1), axis=0)
    left = chosen[:slot_count]
    right = chosen[slot_count:]
    left_t = jnp.transpose(left, (0, 2, 1)).reshape((slot_count, side, side, rows, spec_rows))
    left_t = jnp.where(first_core, jnp.swapaxes(left_t, 1, 2), left_t)
    packed_rows = spec_rows * side * rows // block_width
    packs = jnp.transpose(left_t, (1, 0, 2, 3, 4)).reshape(
        (side, slot_count, packed_rows, block_width)
    )

    def rows_for(pos):
        return lax.dynamic_index_in_dim(packs, pos, 0, keepdims=False)

    def gather_perm(d):
        perm = []
        for p in range(pairs_count):
            for z in range(side):
                for y in range(side):
                    src = (p * side + z) * side + y
                    if p % 2 == 0:
                        dst = (p * side + z) * side + (y + d) % side
                    else:
                        dst = (p * side + (z + d) % side) * side + y
                    perm.append((src, dst))
        return perm

    def reduce_perm(e):
        perm = []
        for p in range(pairs_count):
            for z in range(side):
                for y in range(side):
                    src = (p * side + z) * side + y
                    if p % 2 == 0:
                        dst = (p * side + (z + e) % side) * side + y
                    else:
                        dst = (p * side + z) * side + (y + e) % side
                    perm.append((src, dst))
        return perm

    axes = ("pairs", "z", "y")
    pieces = [jnp.concatenate([right, rows_for(gather_pos)], axis=1)]
    for d in sorted(range(1, side), key=lambda step: -min(step, side - step)):
        message = jnp.concatenate([right, rows_for((gather_pos + d) % side)], axis=1)
        pieces.append(lax.ppermute(message, axes, gather_perm(d)))
    gathered = jnp.stack(pieces)
    right_all = gathered[:, :, :spec_rows].reshape(
        (side, slot_count, seg_dev, 2, FREQS, block_width)
    )
    left_all = gathered[:, :, spec_rows:].reshape((side, slot_count, side * rows, seg_dev, 2, FREQS))
    left_all = jnp.transpose(left_all, (0, 1, 3, 4, 5, 2))
    right_swapped = jnp.stack([right_all[:, :, :, 1], -right_all[:, :, :, 0]], axis=3)
    rhs = jnp.concatenate([right_all, right_swapped], axis=-1)
    partial_value = jnp.einsum(
        "akscfm,akscfn->kfmn", left_all, rhs, preferred_element_type=jnp.float32
    )
    partial_value = partial_value.reshape((slot_count, FREQS, side, rows, 2, block_width))
    partial_value = jnp.transpose(partial_value, (2, 0, 4, 1, 3, 5)).astype(jnp.bfloat16)
    chunk_rows = slot_count * 2 * FREQS * rows
    partial_value = partial_value.reshape((side, chunk_rows, block_width))
    stacked = lax.dynamic_index_in_dim(partial_value, reduce_pos, 0, keepdims=False).astype(
        jnp.float32
    )
    for e in sorted(range(1, side), key=lambda step: -min(step, side - step)):
        chunk = lax.dynamic_index_in_dim(partial_value, (reduce_pos + e) % side, 0, keepdims=False)
        stacked = stacked + lax.ppermute(chunk, axes, reduce_perm(e)).astype(jnp.float32)
    stacked = stacked.reshape((slot_count, 2, FREQS, rows, block_width))
    lag_weights = lag_table(seg_dev * side * side).reshape(2, FREQS, LAGS)
    correlation = jnp.einsum(
        "kpfrj,pft->krjt",
        stacked,
        lag_weights,
        precision=lax.Precision.DEFAULT,
        preferred_element_type=jnp.float32,
    )
    masked = correlation * live_slots.astype(jnp.float32)[:, None, None, None]
    return masked.astype(jnp.bfloat16)[None]


def solution(mesh):
    pairs_count, win_count = mesh.devices.shape
    side = math.isqrt(win_count)
    grid = Mesh(mesh.devices.reshape(pairs_count, side, side), ("pairs", "z", "y"))
    in_specs = (P("pairs", ("z", "y"), None, None), P(), P())
    out_specs = P("pairs", None, ("z", "y"), None, None)
    return jax.shard_map(shards, mesh=grid, in_specs=in_specs, out_specs=out_specs, check_vma=False)
```

```python
import math

import jax
import jax.numpy as jnp
import ml_dtypes
import numpy as np
from jax import lax
from jax.sharding import Mesh
from jax.sharding import PartitionSpec as P

NSAMP = 4096
FREQS = 32
LOW_BIN = 16
LAGS = 128


WATER = 0.1


def band_table():
    sample_idx = np.arange(NSAMP, dtype=np.int64)
    bin_idx = np.arange(FREQS, dtype=np.int64) + LOW_BIN
    phase = (sample_idx[:, None] * bin_idx[None, :] % NSAMP).astype(np.float64) * (
        2.0 * math.pi / NSAMP
    )
    scaled = np.concatenate([np.cos(phase), -np.sin(phase)], axis=1) * (1.0 / math.sqrt(NSAMP))
    return jnp.asarray(scaled.astype(ml_dtypes.bfloat16))


def lag_table(segments):
    bin_idx = np.arange(FREQS, dtype=np.int64) + LOW_BIN
    lag_idx = (np.arange(LAGS, dtype=np.int64) - LAGS // 2) * (NSAMP // LAGS)
    phase = (bin_idx[:, None] * lag_idx[None, :] % NSAMP).astype(np.float32) * np.float32(
        2.0 * math.pi / NSAMP
    )
    table = np.concatenate([np.cos(phase), -np.sin(phase)], axis=0) * np.float32(
        1.0 / math.sqrt(segments * FREQS)
    )
    return jnp.asarray(table.astype(np.float32))


def whiten(spectra):
    real_part = spectra[..., :FREQS]
    imag_part = spectra[..., FREQS:]
    power_bins = real_part * real_part + imag_part * imag_part
    widths = [(0, 0)] * (power_bins.ndim - 1) + [(2, 2)]
    padded = jnp.pad(power_bins, widths)
    smooth = (
        padded[..., 0:FREQS]
        + padded[..., 1 : FREQS + 1]
        + padded[..., 2 : FREQS + 2]
        + padded[..., 3 : FREQS + 3]
        + padded[..., 4 : FREQS + 4]
    ) * 0.2
    water_level = smooth + WATER * jnp.mean(power_bins, axis=-1, keepdims=True) + 1e-06
    factor = lax.rsqrt(water_level)
    return jnp.concatenate([real_part * factor, imag_part * factor], axis=-1).astype(jnp.bfloat16)


def shards(records, pair_list, pair_count):
    seg_dev = records.shape[1]
    block_width = records.shape[2]
    slot_count = pair_list.shape[1]
    pairs_count = lax.axis_size("pairs")
    side = lax.axis_size("y")
    rows = block_width // (side * side)
    chips = pairs_count // 2
    width = 2 * FREQS
    spec_rows = seg_dev * width
    half_rows = spec_rows // 2
    spectra = whiten(jnp.dot(records[0], band_table(), preferred_element_type=jnp.float32))
    own = jnp.transpose(spectra, (0, 2, 1)).reshape(spec_rows, block_width)
    owner_index = lax.axis_index("pairs")
    core = owner_index % 2
    chip = owner_index // 2
    first_core = core == 0
    z_index = lax.axis_index("z")
    y_index = lax.axis_index("y")
    gather_pos = jnp.where(first_core, y_index, z_index)
    reduce_pos = jnp.where(first_core, z_index, y_index)

    swap = [(p, p ^ 1) for p in range(pairs_count)]

    def chip_shift(d):
        return [(p, 2 * ((p // 2 + d) % chips) + p % 2) for p in range(pairs_count)]

    partner = lax.ppermute(own, "pairs", swap)
    from_below = lax.ppermute(own, "pairs", chip_shift(1))
    from_above = lax.ppermute(own, "pairs", chip_shift(-1))
    from_far = lax.ppermute(own, "pairs", chip_shift(2))
    mine = jnp.stack([own, from_above, from_far, from_below])
    theirs_near = lax.ppermute(jnp.stack([from_above, from_below]), "pairs", swap)
    theirs_far = lax.ppermute(from_far, "pairs", swap)
    theirs = jnp.stack([partner, theirs_near[0], theirs_far, theirs_near[1]])
    table = jnp.where(
        first_core, jnp.stack([mine, theirs], axis=1), jnp.stack([theirs, mine], axis=1)
    ).reshape((pairs_count,) + own.shape)
    own_pairs = lax.dynamic_index_in_dim(pair_list, owner_index, 0, keepdims=False)
    live_slots = jnp.arange(slot_count, dtype=jnp.int32) < pair_count[owner_index]
    position = ((own_pairs // 2 - chip) % chips) * 2 + own_pairs % 2
    chosen = jnp.take(table, position.T.reshape(-1), axis=0)
    left = chosen[:slot_count]
    right = chosen[slot_count:]
    left_t = jnp.transpose(left, (0, 2, 1)).reshape((slot_count, side, side, rows, spec_rows))
    left_t = jnp.where(first_core, jnp.swapaxes(left_t, 1, 2), left_t)
    packed_rows = spec_rows * side * rows // block_width
    packs = jnp.transpose(left_t, (1, 0, 2, 3, 4)).reshape(
        (side, slot_count, packed_rows, block_width)
    )

    def rows_for(pos):
        return lax.dynamic_index_in_dim(packs, pos, 0, keepdims=False)

    def gather_perm(d):
        perm = []
        for p in range(pairs_count):
            for z in range(side):
                for y in range(side):
                    src = (p * side + z) * side + y
                    if p % 2 == 0:
                        dst = (p * side + z) * side + (y + d) % side
                    else:
                        dst = (p * side + (z + d) % side) * side + y
                    perm.append((src, dst))
        return perm

    def reduce_perm(e):
        perm = []
        for p in range(pairs_count):
            for z in range(side):
                for y in range(side):
                    src = (p * side + z) * side + y
                    if p % 2 == 0:
                        dst = (p * side + (z + e) % side) * side + y
                    else:
                        dst = (p * side + z) * side + (y + e) % side
                    perm.append((src, dst))
        return perm

    axes = ("pairs", "z", "y")
    pieces = [jnp.concatenate([right, rows_for(gather_pos)], axis=1)]
    for d in sorted(range(1, side), key=lambda step: -min(step, side - step)):
        message = jnp.concatenate([right, rows_for((gather_pos + d) % side)], axis=1)
        pieces.append(lax.ppermute(message, axes, gather_perm(d)))
    gathered = jnp.stack(pieces)
    right_all = gathered[:, :, :spec_rows].reshape(
        (side, slot_count, seg_dev, 2, FREQS, block_width)
    )
    left_all = gathered[:, :, spec_rows:].reshape((side, slot_count, side * rows, seg_dev, 2, FREQS))
    left_all = jnp.transpose(left_all, (0, 1, 3, 4, 5, 2))
    right_swapped = jnp.stack([right_all[:, :, :, 1], -right_all[:, :, :, 0]], axis=3)
    rhs = jnp.concatenate([right_all, right_swapped], axis=-1)
    partial_value = jnp.einsum(
        "akscfm,akscfn->kfmn", left_all, rhs, preferred_element_type=jnp.float32
    )
    partial_value = partial_value.reshape((slot_count, FREQS, side, rows, 2, block_width))
    partial_value = jnp.transpose(partial_value, (2, 0, 4, 1, 3, 5)).astype(jnp.bfloat16)
    chunk_rows = slot_count * 2 * FREQS * rows
    partial_value = partial_value.reshape((side, chunk_rows, block_width))
    stacked = lax.dynamic_index_in_dim(partial_value, reduce_pos, 0, keepdims=False).astype(
        jnp.float32
    )
    for e in sorted(range(1, side), key=lambda step: -min(step, side - step)):
        chunk = lax.dynamic_index_in_dim(partial_value, (reduce_pos + e) % side, 0, keepdims=False)
        stacked = stacked + lax.ppermute(chunk, axes, reduce_perm(e)).astype(jnp.float32)
    stacked = stacked.reshape((slot_count, 2, FREQS, rows, block_width))
    lag_weights = lag_table(seg_dev * side * side).reshape(2, FREQS, LAGS)
    correlation = jnp.einsum(
        "kpfrj,pft->krjt",
        stacked,
        lag_weights,
        precision=lax.Precision.DEFAULT,
        preferred_element_type=jnp.float32,
    )
    masked = correlation * live_slots.astype(jnp.float32)[:, None, None, None]
    return masked.astype(jnp.bfloat16)[None]


def solution(mesh):
    pairs_count, win_count = mesh.devices.shape
    side = math.isqrt(win_count)
    grid = Mesh(mesh.devices.reshape(pairs_count, side, side), ("pairs", "z", "y"))
    in_specs = (P("pairs", ("z", "y"), None, None), P(), P())
    out_specs = P("pairs", None, ("z", "y"), None, None)
    return jax.shard_map(shards, mesh=grid, in_specs=in_specs, out_specs=out_specs, check_vma=False)
```
